32 devices in a mesh: parts: 2 (over y), seq: 4 (over z), lat: 4 (over x, core).
Axes of the slice: x: 2, y: 2, z: 4, core: 2. Of those that a mesh axis runs over, the one named last changes fastest.
Arguments:
- layer_input: bfloat16 [8, 2048, 1024], P(('parts', 'lat'), 'seq'), parts along dimension 0, may hold values from -6 to 6
- query_rows: bfloat16 [8, 2048, 1024], P(('parts', 'lat'), 'seq'), parts along dimension 0, may hold values from -8 to 8, as said below
- key_rows: bfloat16 [8, 2048, 256], P(('parts', 'lat'), 'seq'), parts along dimension 0, may hold values from -8 to 8, as said below
- value_rows: bfloat16 [8, 2048, 256], P(('parts', 'lat'), 'seq'), parts along dimension 0, may hold values from -6 to 6
- saved_output: bfloat16 [8, 2048, 1024], P(('parts', 'lat'), 'seq'), parts along dimension 0, may hold values from -6 to 6
- output_grad: bfloat16 [8, 2048, 1024], P(('parts', 'lat'), 'seq'), parts along dimension 0, may hold values from -96 to 96
- weight_query: bfloat16 [1024, 1024], replicated, may hold values from -0.1875 to 0.1875
- weight_key: bfloat16 [1024, 256], replicated, may hold values from -0.1875 to 0.1875
- weight_value: bfloat16 [1024, 256], replicated, may hold values from -0.1875 to 0.1875
Outputs:
- input_grad: bfloat16 [8, 2048, 1024], P(('parts', 'lat'), 'seq'), parts along dimension 0
- query_weight_grad: float32 [2048, 1024], P(('parts', 'seq', 'lat')), parts along dimension 0
- key_weight_grad: float32 [2048, 256], P(('parts', 'seq', 'lat')), parts along dimension 0
- value_weight_grad: float32 [2048, 256], P(('parts', 'seq', 'lat')), parts along dimension 0
The draws below stay inside these ranges and needn't reach their ends.
There are 2 independent parts, one for each index of `parts`. The reference program is written for one: setup_inputs(seed, part) draws one part's arguments, and reference() takes and returns one part's arrays. A program takes and returns all parts, laid end to end along the dimension named above; an argument that names none is the same for every part. Nothing has to cross between parts.
Inputs may be any that keep to these rules, and one draw needn't show every extreme that they name: `query_rows`: saved queries of the layer. `key_rows`: saved keys of the layer.
All inputs are finite; a program needn't handle non-finite values.
Results may differ from the reference program's by a relative error of at most 0.0055.
Values may be sent and summed in bfloat16 or wider, within the bound.
No kernel may reach another device: no remote copies, remote signals or barrier semaphores. Data moves between devices by JAX's collectives and lax.ppermute only.
A program may use at most 128 MiB of HBM per device.

```python
import jax
import jax.numpy as jnp
from jax import lax

D = 1024
HEADS = 16
HEAD_DIM = 64
KV_HEADS = 4
WINDOW = 512
TOK_DEV = 512
LENGTH = 2048
GROUPS = 4


def attention_pair(key):
    base = jax.random.fold_in(key, 4099)
    key_query, key_keys = jax.random.split(base, 2)
    query_shape = (GROUPS, LENGTH, HEADS * HEAD_DIM)
    keys_shape = (GROUPS, LENGTH, KV_HEADS * HEAD_DIM)
    query_vals = jnp.clip(jax.random.normal(key_query, query_shape, jnp.float32), -5.5, 5.5)
    key_vals = jnp.clip(jax.random.normal(key_keys, keys_shape, jnp.float32), -5.5, 5.5)
    return (query_vals, key_vals)


def draw_query_rows(key, part):
    return attention_pair(key)[0].astype(jnp.bfloat16)


def draw_key_rows(key, part):
    return attention_pair(key)[1].astype(jnp.bfloat16)


def with_spikes(drawn, stream_key, source, target, parts, factor):
    owner, partner = [(jnp.arange(drawn.shape[dim]) // (drawn.shape[dim] // parts)).reshape([-1 if axis == dim else 1 for axis in range(drawn.ndim)]) for dim in (source, target)]
    chosen = jax.random.permutation(stream_key, parts)[partner]
    strong = (owner == chosen) | (owner == (partner + parts // 2) % parts)
    return jnp.where(strong, factor * drawn, drawn)


def levels(stream_key, shape, shards, least, top_value):
    loudness = 1.0
    for axis_at, parts in shards:
        heights = jax.random.uniform(jax.random.fold_in(jax.random.fold_in(stream_key, 6), axis_at), (parts,), jnp.float32, least / len(shards), top_value / len(shards))
        loudness = loudness * jnp.repeat(jnp.exp(heights), shape[axis_at] // parts).reshape((-1,) + (1,) * (len(shape) - 1 - axis_at))
    return loudness


def scatter_about(rng, extent, deviation, most, cuts=(), held_as=jnp.bfloat16):
    entries = deviation * jax.random.normal(rng, extent, jnp.float32)
    if cuts:
        entries = entries * levels(rng, extent, cuts, -0.22, 0.18)
    return jnp.clip(entries, -most, most).astype(held_as)


def bell_draw_with(stream_key, shape, spread, most, pieces, heavy, kind=jnp.bfloat16):
    entries = spread * jax.random.normal(stream_key, shape, jnp.float32)
    if pieces:
        entries = entries * levels(stream_key, shape, pieces, -0.22, 0.18)
    return jnp.clip(with_spikes(entries, jax.random.fold_in(stream_key, 3), *heavy), -most, most).astype(kind)


def setup_inputs(seed: int = 0, part: int = 0) -> dict:
    key_of = jax.random.split(jax.random.key(seed), 10)
    part_splits = jax.random.split(jax.random.fold_in(key_of[9], part), 10)
    layer_input = bell_draw_with(part_splits[0], (GROUPS, LENGTH, D), 1.0, 6.0, ((0, 4), (1, 4)), (1, 2, 4, 2.0))
    query_rows = draw_query_rows(jax.random.fold_in(jax.random.fold_in(key_of[9], part), 71), part)
    key_rows = draw_key_rows(jax.random.fold_in(jax.random.fold_in(key_of[9], part), 71), part)
    value_rows = scatter_about(part_splits[3], (GROUPS, LENGTH, KV_HEADS * HEAD_DIM), 1.0, 6.0, ((0, 4), (1, 4)))
    saved_output = scatter_about(part_splits[4], (GROUPS, LENGTH, HEADS * HEAD_DIM), 1.0, 6.0, ((0, 4), (1, 4)))
    output_grad = scatter_about(part_splits[5], (GROUPS, LENGTH, HEADS * HEAD_DIM), 16.0, 96.0, ((0, 4), (1, 4)))
    weight_query = scatter_about(key_of[6], (D, HEADS * HEAD_DIM), D ** -0.5, 0.1875)
    weight_key = scatter_about(key_of[7], (D, KV_HEADS * HEAD_DIM), D ** -0.5, 0.1875)
    weight_value = scatter_about(key_of[8], (D, KV_HEADS * HEAD_DIM), D ** -0.5, 0.1875)
    return {"layer_input": layer_input, "query_rows": query_rows, "key_rows": key_rows, "value_rows": value_rows, "saved_output": saved_output, "output_grad": output_grad, "weight_query": weight_query, "weight_key": weight_key, "weight_value": weight_value}


def group_terms(query_part, output_part, dout_part, key_part, value_part):
    rows = query_part.shape[0]
    span = key_part.shape[0]
    ratio = HEADS // KV_HEADS
    scale = HEAD_DIM ** -0.5
    queries3 = query_part.reshape(rows, ratio, HEAD_DIM).astype(jnp.float32)
    outputs3 = output_part.reshape(rows, ratio, HEAD_DIM).astype(jnp.float32)
    douts3 = dout_part.reshape(rows, ratio, HEAD_DIM).astype(jnp.float32)
    keys_flt = key_part.astype(jnp.float32)
    values_flt = value_part.astype(jnp.float32)
    scores = jnp.einsum("qrd,kd->rqk", queries3, keys_flt) * scale
    row_index = jnp.arange(rows, dtype=jnp.int32)[:, None]
    col_index = jnp.arange(span, dtype=jnp.int32)[None, :]
    linked = (col_index > row_index) & (col_index <= row_index + WINDOW)
    scores = jnp.where(linked[None], scores, -jnp.inf)
    peak = jnp.max(scores, axis=-1, keepdims=True)
    raised = jnp.exp(scores - peak)
    probs = raised / jnp.sum(raised, axis=-1, keepdims=True)
    probs_low = lax.optimization_barrier(probs.astype(jnp.bfloat16)).astype(jnp.float32)
    dprobs = jnp.einsum("qrd,kd->rqk", douts3, values_flt)
    delta = jnp.sum(douts3 * outputs3, axis=-1).T[:, :, None]
    dscores = lax.optimization_barrier((probs * (dprobs - delta)).astype(jnp.bfloat16)).astype(jnp.float32)
    query_grad = jnp.einsum("rqk,kd->qrd", dscores, keys_flt) * scale
    key_grad = jnp.einsum("rqk,qrd->kd", dscores, queries3) * scale
    value_grad = jnp.einsum("rqk,qrd->kd", probs_low, douts3)
    return query_grad.reshape(rows, ratio * HEAD_DIM), key_grad, value_grad


def block_terms(query_blk, output_blk, dout_blk, key_blk, value_blk):
    width = (HEADS // KV_HEADS) * HEAD_DIM
    query_list, key_list, value_list = [], [], []
    for group in range(KV_HEADS):
        cols = slice(group * width, (group + 1) * width)
        kv_cols = slice(group * HEAD_DIM, (group + 1) * HEAD_DIM)
        q_term, k_term, v_term = group_terms(query_blk[:, cols], output_blk[:, cols], dout_blk[:, cols], key_blk[:, kv_cols], value_blk[:, kv_cols])
        query_list.append(q_term)
        key_list.append(k_term)
        value_list.append(v_term)
    return jnp.concatenate(query_list, 1), jnp.concatenate(key_list, 1), jnp.concatenate(value_list, 1)


def reference(layer_input, query_rows, key_rows, value_rows, saved_output, output_grad, weight_query, weight_key, weight_value):
    block = min(512, TOK_DEV)
    kv_width = KV_HEADS * HEAD_DIM

    def one_group(arrays):
        queries, keys_all, values_all, outputs_all, douts = arrays
        length = queries.shape[0]
        ext_keys = jnp.concatenate([keys_all[length - WINDOW:], keys_all], axis=0)
        ext_values = jnp.concatenate([values_all[length - WINDOW:], values_all], axis=0)

        def advance(carry, block_id):
            key_acc, value_acc = carry
            start = (block_id * block).astype(jnp.int32)
            query_blk = lax.dynamic_slice_in_dim(queries, start, block, 0)
            output_blk = lax.dynamic_slice_in_dim(outputs_all, start, block, 0)
            dout_blk = lax.dynamic_slice_in_dim(douts, start, block, 0)
            key_blk = lax.dynamic_slice_in_dim(ext_keys, start, block + WINDOW, 0)
            value_blk = lax.dynamic_slice_in_dim(ext_values, start, block + WINDOW, 0)
            q_term, k_term, v_term = block_terms(query_blk, output_blk, dout_blk, key_blk, value_blk)
            key_acc = lax.dynamic_update_slice_in_dim(key_acc, lax.dynamic_slice_in_dim(key_acc, start, block + WINDOW, 0) + k_term, start, 0)
            value_acc = lax.dynamic_update_slice_in_dim(value_acc, lax.dynamic_slice_in_dim(value_acc, start, block + WINDOW, 0) + v_term, start, 0)
            return (key_acc, value_acc), q_term.astype(jnp.bfloat16)

        zero_acc = jnp.zeros((length + WINDOW, kv_width), jnp.float32)
        (key_acc, value_acc), query_blocks = lax.scan(advance, (zero_acc, zero_acc), jnp.arange(length // block, dtype=jnp.int32))
        query_grad = query_blocks.reshape(length, HEADS * HEAD_DIM)
        key_grad = key_acc[WINDOW:].at[length - WINDOW:].add(key_acc[:WINDOW]).astype(jnp.bfloat16)
        value_grad = value_acc[WINDOW:].at[length - WINDOW:].add(value_acc[:WINDOW]).astype(jnp.bfloat16)
        return query_grad, key_grad, value_grad

    query_grad, key_grad, value_grad = lax.map(one_group, (query_rows, key_rows, value_rows, saved_output, output_grad))
    tokens = GROUPS * LENGTH
    query_flat = query_grad.reshape(tokens, HEADS * HEAD_DIM)
    key_flat = key_grad.reshape(tokens, kv_width)
    value_flat = value_grad.reshape(tokens, kv_width)
    input_flat = layer_input.reshape(tokens, D)
    summed = jnp.dot(query_flat, weight_query.T, preferred_element_type=jnp.float32)
    summed = summed + jnp.dot(key_flat, weight_key.T, preferred_element_type=jnp.float32)
    summed = summed + jnp.dot(value_flat, weight_value.T, preferred_element_type=jnp.float32)
    input_grad = summed.astype(jnp.bfloat16).reshape(GROUPS, LENGTH, D)
    query_weight_grad = jnp.dot(input_flat.T, query_flat, preferred_element_type=jnp.float32)
    key_weight_grad = jnp.dot(input_flat.T, key_flat, preferred_element_type=jnp.float32)
    value_weight_grad = jnp.dot(input_flat.T, value_flat, preferred_element_type=jnp.float32)
    return (input_grad, query_weight_grad, key_weight_grad, value_weight_grad)
```

```python
import jax
import jax.numpy as jnp
from jax import lax
from jax.sharding import PartitionSpec as P

HEADS = 16
HEAD_DIM = 64
KV_HEADS = 4
WINDOW = 512


def shifted(block, axis, distance):
    devices = range(lax.axis_size(axis))
    route = [((i - distance) % len(devices), i) for i in devices]
    return lax.ppermute(block, axis, route)


def group_terms(query_part, output_part, dout_part, key_part, value_part):
    rows = query_part.shape[0]
    span = key_part.shape[0]
    ratio = HEADS // KV_HEADS
    scale = HEAD_DIM ** (-0.5)
    queries3 = query_part.reshape(rows, ratio, HEAD_DIM)
    outputs3 = output_part.reshape(rows, ratio, HEAD_DIM)
    douts3 = dout_part.reshape(rows, ratio, HEAD_DIM)
    scores = (
        jnp.einsum("qrd,kd->rqk", queries3, key_part, preferred_element_type=jnp.float32) * scale
    )
    row_index = jnp.arange(rows, dtype=jnp.int32)[:, None]
    col_index = jnp.arange(span, dtype=jnp.int32)[None, :]
    linked = (col_index > row_index) & (col_index <= row_index + WINDOW)
    scores = jnp.where(linked[None], scores, -jnp.inf)
    peak = jnp.max(scores, axis=-1, keepdims=True)
    raised = jnp.exp(scores - peak)
    probs = raised / jnp.sum(raised, axis=-1, keepdims=True)
    probs_low = probs.astype(jnp.bfloat16)
    dprobs = jnp.einsum("qrd,kd->rqk", douts3, value_part, preferred_element_type=jnp.float32)
    delta = jnp.sum(douts3.astype(jnp.float32) * outputs3.astype(jnp.float32), axis=-1).T[
        :, :, None
    ]
    dscores = (probs * (dprobs - delta)).astype(jnp.bfloat16)
    query_grad = (
        jnp.einsum("rqk,kd->qrd", dscores, key_part, preferred_element_type=jnp.float32) * scale
    )
    key_grad = (
        jnp.einsum("rqk,qrd->kd", dscores, queries3, preferred_element_type=jnp.float32) * scale
    )
    value_grad = jnp.einsum("rqk,qrd->kd", probs_low, douts3, preferred_element_type=jnp.float32)
    return (query_grad.reshape(rows, ratio * HEAD_DIM), key_grad, value_grad)


def body(
    layer_input,
    query_rows,
    key_rows,
    value_rows,
    saved_output,
    output_grad,
    weight_query,
    weight_key,
    weight_value,
):
    inputs = layer_input[0]
    queries = query_rows[0]
    keys_own = key_rows[0]
    values_own = value_rows[0]
    outputs_own = saved_output[0]
    douts = output_grad[0]
    tokens = queries.shape[0]
    kv_width = keys_own.shape[1]
    width = HEADS // KV_HEADS * HEAD_DIM
    block = min(512, tokens)
    tail_pair = jnp.stack([keys_own, values_own])
    prior_pair = shifted(tail_pair, "seq", 1)
    ext_keys = jnp.concatenate([prior_pair[0], keys_own], axis=0)
    ext_values = jnp.concatenate([prior_pair[1], values_own], axis=0)
    key_acc = jnp.zeros((tokens + WINDOW, kv_width), jnp.float32)
    value_acc = jnp.zeros((tokens + WINDOW, kv_width), jnp.float32)
    query_list = []
    key_list = []
    value_list = []
    for group in range(KV_HEADS):
        cols = slice(group * width, (group + 1) * width)
        kv_cols = slice(group * HEAD_DIM, (group + 1) * HEAD_DIM)
        q_term, k_term, v_term = group_terms(
            queries[0:block, cols],
            outputs_own[0:block, cols],
            douts[0:block, cols],
            ext_keys[0 : block + WINDOW, kv_cols],
            ext_values[0 : block + WINDOW, kv_cols],
        )
        query_list.append(q_term)
        key_list.append(k_term)
        value_list.append(v_term)
    query_blocks = jnp.concatenate(query_list, 1).astype(jnp.bfloat16)
    key_acc = key_acc.at[0 : block + WINDOW].add(jnp.concatenate(key_list, 1))
    value_acc = value_acc.at[0 : block + WINDOW].add(jnp.concatenate(value_list, 1))
    front_pair = jnp.stack([key_acc[:WINDOW], value_acc[:WINDOW]])
    returned = shifted(front_pair, "seq", -1)
    key_grad = key_acc[WINDOW:].at[tokens - WINDOW :].add(returned[0]).astype(jnp.bfloat16)
    value_grad = value_acc[WINDOW:].at[tokens - WINDOW :].add(returned[1]).astype(jnp.bfloat16)
    contract_cols = (((1,), (1,)), ((), ()))
    summed = lax.dot_general(
        query_blocks, weight_query, contract_cols, preferred_element_type=jnp.float32
    )
    summed = summed + lax.dot_general(
        key_grad, weight_key, contract_cols, preferred_element_type=jnp.float32
    )
    summed = summed + lax.dot_general(
        value_grad, weight_value, contract_cols, preferred_element_type=jnp.float32
    )
    input_grad = summed.astype(jnp.bfloat16)[None]
    all_grads = jnp.concatenate([query_blocks, key_grad, value_grad], axis=1)
    seq_n = lax.axis_size("seq")
    lx_n = lax.axis_size("lx")
    core_n = lax.axis_size("core")
    model = inputs.shape[1]
    rows = model // (seq_n * lx_n * core_n)
    reordered = (
        inputs.reshape(tokens, seq_n, lx_n, core_n, rows)
        .transpose(0, 3, 1, 2, 4)
        .reshape(tokens, model)
    )
    partial = lax.dot_general(
        reordered, all_grads, (((0,), (0,)), ((), ())), preferred_element_type=jnp.float32
    )
    in_chip = lax.psum_scatter(partial, "core", scatter_dimension=0, tiled=True)
    owned = lax.psum_scatter(in_chip, ("seq", "lx"), scatter_dimension=0, tiled=True)
    q_width = HEADS * HEAD_DIM
    query_weight_grad = owned[:, :q_width]
    key_weight_grad = owned[:, q_width : q_width + kv_width]
    value_weight_grad = owned[:, q_width + kv_width :]
    return (input_grad, query_weight_grad, key_weight_grad, value_weight_grad)


def solution(mesh):
    from jax.sharding import Mesh

    grid = mesh.devices
    split = Mesh(
        grid.reshape(grid.shape[0], grid.shape[1], grid.shape[2] // 2, 2),
        ("parts", "seq", "lx", "core"),
    )
    rows_spec = P(("parts", "lx", "core"), "seq", None)
    placed = (rows_spec,) * 6 + (P(), P(), P())
    grads_spec = P(("parts", "seq", "lx", "core"), None)
    return jax.shard_map(
        body,
        mesh=split,
        in_specs=placed,
        out_specs=(rows_spec, grads_spec, grads_spec, grads_spec),
        check_vma=False,
    )
```

```python
import jax
import jax.numpy as jnp
from jax import lax
from jax.sharding import PartitionSpec as P

HEADS = 16
HEAD_DIM = 64
KV_HEADS = 4
WINDOW = 512


def shifted(block, axis, distance):
    devices = range(lax.axis_size(axis))
    route = [((i - distance) % len(devices), i) for i in devices]
    return lax.ppermute(block, axis, route)


def group_terms(query_part, output_part, dout_part, key_part, value_part):
    rows = query_part.shape[0]
    span = key_part.shape[0]
    ratio = HEADS // KV_HEADS
    scale = HEAD_DIM ** (-0.5)
    queries3 = query_part.reshape(rows, ratio, HEAD_DIM)
    outputs3 = output_part.reshape(rows, ratio, HEAD_DIM)
    douts3 = dout_part.reshape(rows, ratio, HEAD_DIM)
    scores = (
        jnp.einsum("qrd,kd->rqk", queries3, key_part, preferred_element_type=jnp.float32) * scale
    )
    row_index = jnp.arange(rows, dtype=jnp.int32)[:, None]
    col_index = jnp.arange(span, dtype=jnp.int32)[None, :]
    linked = (col_index > row_index) & (col_index <= row_index + WINDOW)
    scores = jnp.where(linked[None], scores, -jnp.inf)
    peak = jnp.max(scores, axis=-1, keepdims=True)
    raised = jnp.exp(scores - peak)
    probs = raised / jnp.sum(raised, axis=-1, keepdims=True)
    probs_low = probs.astype(jnp.bfloat16)
    dprobs = jnp.einsum("qrd,kd->rqk", douts3, value_part, preferred_element_type=jnp.float32)
    delta = jnp.sum(douts3.astype(jnp.float32) * outputs3.astype(jnp.float32), axis=-1).T[
        :, :, None
    ]
    dscores = (probs * (dprobs - delta)).astype(jnp.bfloat16)
    query_grad = (
        jnp.einsum("rqk,kd->qrd", dscores, key_part, preferred_element_type=jnp.float32) * scale
    )
    key_grad = (
        jnp.einsum("rqk,qrd->kd", dscores, queries3, preferred_element_type=jnp.float32) * scale
    )
    value_grad = jnp.einsum("rqk,qrd->kd", probs_low, douts3, preferred_element_type=jnp.float32)
    return (query_grad.reshape(rows, ratio * HEAD_DIM), key_grad, value_grad)


def body(
    layer_input,
    query_rows,
    key_rows,
    value_rows,
    saved_output,
    output_grad,
    weight_query,
    weight_key,
    weight_value,
):
    inputs = layer_input[0]
    queries = query_rows[0]
    keys_own = key_rows[0]
    values_own = value_rows[0]
    outputs_own = saved_output[0]
    douts = output_grad[0]
    tokens = queries.shape[0]
    kv_width = keys_own.shape[1]
    width = HEADS // KV_HEADS * HEAD_DIM
    block = min(512, tokens)
    tail_pair = jnp.stack([keys_own, values_own])
    prior_pair = shifted(tail_pair, "seq", 1)
    ext_keys = jnp.concatenate([prior_pair[0], keys_own], axis=0)
    ext_values = jnp.concatenate([prior_pair[1], values_own], axis=0)
    fronts = []
    owns = []
    query_list = []
    wq_list = []
    for group in range(KV_HEADS):
        cols = slice(group * width, (group + 1) * width)
        kv_cols = slice(group * HEAD_DIM, (group + 1) * HEAD_DIM)
        q_term, k_term, v_term = group_terms(
            queries[0:block, cols],
            outputs_own[0:block, cols],
            douts[0:block, cols],
            ext_keys[0 : block + WINDOW, kv_cols],
            ext_values[0 : block + WINDOW, kv_cols],
        )
        q_low = q_term.astype(jnp.bfloat16)
        query_list.append(q_low)
        wq_part = lax.dot_general(
            inputs, q_low, (((0,), (0,)), ((), ())), preferred_element_type=jnp.float32
        )
        wq_list.append(
            lax.psum_scatter(wq_part, ("seq", "lat"), scatter_dimension=0, tiled=True)
        )
        fronts.append(shifted(jnp.stack([k_term[:WINDOW], v_term[:WINDOW]]), "seq", -1))
        owns.append((k_term[WINDOW:], v_term[WINDOW:]))
    query_blocks = jnp.concatenate(query_list, 1)
    key_grad = jnp.concatenate(
        [own[0].at[tokens - WINDOW :].add(back[0]) for own, back in zip(owns, fronts)], 1
    ).astype(jnp.bfloat16)
    value_grad = jnp.concatenate(
        [own[1].at[tokens - WINDOW :].add(back[1]) for own, back in zip(owns, fronts)], 1
    ).astype(jnp.bfloat16)
    contract_cols = (((1,), (1,)), ((), ()))
    summed = lax.dot_general(
        query_blocks, weight_query, contract_cols, preferred_element_type=jnp.float32
    )
    summed = summed + lax.dot_general(
        key_grad, weight_key, contract_cols, preferred_element_type=jnp.float32
    )
    summed = summed + lax.dot_general(
        value_grad, weight_value, contract_cols, preferred_element_type=jnp.float32
    )
    input_grad = summed.astype(jnp.bfloat16)[None]
    kv_grads = jnp.concatenate([key_grad, value_grad], axis=1)
    kv_owned = lax.psum_scatter(
        lax.dot_general(
            inputs, kv_grads, (((0,), (0,)), ((), ())), preferred_element_type=jnp.float32
        ),
        ("seq", "lat"),
        scatter_dimension=0,
        tiled=True,
    )
    query_weight_grad = jnp.concatenate(wq_list, 1)
    key_weight_grad = kv_owned[:, :kv_width]
    value_weight_grad = kv_owned[:, kv_width:]
    return (input_grad, query_weight_grad, key_weight_grad, value_weight_grad)


def solution(mesh):
    placed = (
        P(("parts", "lat"), "seq", None),
        P(("parts", "lat"), "seq", None),
        P(("parts", "lat"), "seq", None),
        P(("parts", "lat"), "seq", None),
        P(("parts", "lat"), "seq", None),
        P(("parts", "lat"), "seq", None),
        P(),
        P(),
        P(),
    )
    return jax.shard_map(
        body,
        mesh=mesh,
        in_specs=placed,
        out_specs=(
            P(("parts", "lat"), "seq", None),
            P(("parts", "seq", "lat"), None),
            P(("parts", "seq", "lat"), None),
            P(("parts", "seq", "lat"), None),
        ),
        check_vma=False,
    )
```

```python
import jax
import jax.numpy as jnp
from jax import lax
from jax.sharding import PartitionSpec as P

HEADS = 16
HEAD_DIM = 64
KV_HEADS = 4
WINDOW = 512


def shifted(block, axis, distance):
    devices = range(lax.axis_size(axis))
    route = [((i - distance) % len(devices), i) for i in devices]
    return lax.ppermute(block, axis, route)


def group_terms(query_part, output_part, dout_part, key_part, value_part):
    rows = query_part.shape[0]
    span = key_part.shape[0]
    ratio = HEADS // KV_HEADS
    scale = HEAD_DIM ** (-0.5)
    queries3 = query_part.reshape(rows, ratio, HEAD_DIM)
    outputs3 = output_part.reshape(rows, ratio, HEAD_DIM)
    douts3 = dout_part.reshape(rows, ratio, HEAD_DIM)
    scores = (
        jnp.einsum("qrd,kd->rqk", queries3, key_part, preferred_element_type=jnp.float32) * scale
    )
    row_index = jnp.arange(rows, dtype=jnp.int32)[:, None]
    col_index = jnp.arange(span, dtype=jnp.int32)[None, :]
    linked = (col_index > row_index) & (col_index <= row_index + WINDOW)
    scores = jnp.where(linked[None], scores, -jnp.inf)
    peak = jnp.max(scores, axis=-1, keepdims=True)
    raised = jnp.exp(scores - peak)
    probs = raised / jnp.sum(raised, axis=-1, keepdims=True)
    probs_low = probs.astype(jnp.bfloat16)
    dprobs = jnp.einsum("qrd,kd->rqk", douts3, value_part, preferred_element_type=jnp.float32)
    delta = jnp.sum(douts3.astype(jnp.float32) * outputs3.astype(jnp.float32), axis=-1).T[
        :, :, None
    ]
    dscores = (probs * (dprobs - delta)).astype(jnp.bfloat16)
    query_grad = (
        jnp.einsum("rqk,kd->qrd", dscores, key_part, preferred_element_type=jnp.float32) * scale
    )
    key_grad = (
        jnp.einsum("rqk,qrd->kd", dscores, queries3, preferred_element_type=jnp.float32) * scale
    )
    value_grad = jnp.einsum("rqk,qrd->kd", probs_low, douts3, preferred_element_type=jnp.float32)
    return (query_grad.reshape(rows, ratio * HEAD_DIM), key_grad, value_grad)


def body(
    layer_input,
    query_rows,
    key_rows,
    value_rows,
    saved_output,
    output_grad,
    weight_query,
    weight_key,
    weight_value,
):
    inputs = layer_input[0]
    queries = query_rows[0]
    keys_own = key_rows[0]
    values_own = value_rows[0]
    outputs_own = saved_output[0]
    douts = output_grad[0]
    tokens = queries.shape[0]
    kv_width = keys_own.shape[1]
    width = HEADS // KV_HEADS * HEAD_DIM
    block = min(512, tokens)
    tail_pair = jnp.stack([keys_own, values_own])
    prior_pair = shifted(tail_pair, "seq", 1)
    prior_inputs = shifted(inputs, "seq", 1)
    ext_keys = jnp.concatenate([prior_pair[0], keys_own], axis=0)
    ext_values = jnp.concatenate([prior_pair[1], values_own], axis=0)
    key_acc = jnp.zeros((tokens + WINDOW, kv_width), jnp.float32)
    value_acc = jnp.zeros((tokens + WINDOW, kv_width), jnp.float32)
    query_list = []
    key_list = []
    value_list = []
    for group in range(KV_HEADS):
        cols = slice(group * width, (group + 1) * width)
        kv_cols = slice(group * HEAD_DIM, (group + 1) * HEAD_DIM)
        q_term, k_term, v_term = group_terms(
            queries[0:block, cols],
            outputs_own[0:block, cols],
            douts[0:block, cols],
            ext_keys[0 : block + WINDOW, kv_cols],
            ext_values[0 : block + WINDOW, kv_cols],
        )
        query_list.append(q_term)
        key_list.append(k_term)
        value_list.append(v_term)
    query_blocks = jnp.concatenate(query_list, 1).astype(jnp.bfloat16)
    key_acc = key_acc.at[0 : block + WINDOW].add(jnp.concatenate(key_list, 1))
    value_acc = value_acc.at[0 : block + WINDOW].add(jnp.concatenate(value_list, 1))
    front_pair = jnp.stack([key_acc[:WINDOW], value_acc[:WINDOW]])
    returned = shifted(front_pair, "seq", -1)
    key_grad = key_acc[WINDOW:].at[tokens - WINDOW :].add(returned[0]).astype(jnp.bfloat16)
    value_grad = value_acc[WINDOW:].at[tokens - WINDOW :].add(returned[1]).astype(jnp.bfloat16)
    contract_cols = (((1,), (1,)), ((), ()))
    summed = lax.dot_general(
        query_blocks, weight_query, contract_cols, preferred_element_type=jnp.float32
    )
    summed = summed + lax.dot_general(
        key_grad, weight_key, contract_cols, preferred_element_type=jnp.float32
    )
    summed = summed + lax.dot_general(
        value_grad, weight_value, contract_cols, preferred_element_type=jnp.float32
    )
    input_grad = summed.astype(jnp.bfloat16)[None]
    own_grads = jnp.concatenate(
        [query_blocks, key_acc[WINDOW:].astype(jnp.bfloat16), value_acc[WINDOW:].astype(jnp.bfloat16)],
        axis=1,
    )
    front_grads = jnp.concatenate(
        [key_acc[:WINDOW].astype(jnp.bfloat16), value_acc[:WINDOW].astype(jnp.bfloat16)], axis=1
    )
    by_tokens = (((0,), (0,)), ((), ()))
    partial = lax.dot_general(inputs, own_grads, by_tokens, preferred_element_type=jnp.float32)
    front_part = lax.dot_general(
        prior_inputs[tokens - WINDOW :], front_grads, by_tokens, preferred_element_type=jnp.float32
    )
    q_span = query_blocks.shape[1]
    partial = partial.at[:, q_span:].add(front_part)
    owned = lax.psum_scatter(partial, ("seq", "lat"), scatter_dimension=0, tiled=True)
    q_width = HEADS * HEAD_DIM
    query_weight_grad = owned[:, :q_width]
    key_weight_grad = owned[:, q_width : q_width + kv_width]
    value_weight_grad = owned[:, q_width + kv_width :]
    return (input_grad, query_weight_grad, key_weight_grad, value_weight_grad)


def solution(mesh):
    placed = (
        P(("parts", "lat"), "seq", None),
        P(("parts", "lat"), "seq", None),
        P(("parts", "lat"), "seq", None),
        P(("parts", "lat"), "seq", None),
        P(("parts", "lat"), "seq", None),
        P(("parts", "lat"), "seq", None),
        P(),
        P(),
        P(),
    )
    return jax.shard_map(
        body,
        mesh=mesh,
        in_specs=placed,
        out_specs=(
            P(("parts", "lat"), "seq", None),
            P(("parts", "seq", "lat"), None),
            P(("parts", "seq", "lat"), None),
            P(("parts", "seq", "lat"), None),
        ),
        check_vma=False,
    )
```

```python
import jax
import jax.numpy as jnp
from jax import lax
from jax.experimental import pallas as pl
from jax.sharding import PartitionSpec as P

HEADS = 16
HEAD_DIM = 64
KV_HEADS = 4
WINDOW = 512


def shifted(block, axis, distance):
    devices = range(lax.axis_size(axis))
    route = [((i - distance) % len(devices), i) for i in devices]
    return lax.ppermute(block, axis, route)


def attn_kernel(q_ref, o_ref, do_ref, k_ref, v_ref, dq_ref, dk_ref, dv_ref):
    rows = q_ref.shape[0]
    span = k_ref.shape[1]
    ratio = HEADS // KV_HEADS
    scale = HEAD_DIM ** (-0.5)
    keys = k_ref[0]
    values = v_ref[0]
    row = lax.broadcasted_iota(jnp.int32, (rows, span), 0)
    col = lax.broadcasted_iota(jnp.int32, (rows, span), 1)
    linked = (col > row) & (col <= row + WINDOW)
    by_rows = (((0,), (0,)), ((), ()))
    by_cols = (((1,), (1,)), ((), ()))
    dk = jnp.zeros((span, HEAD_DIM), jnp.float32)
    dv = jnp.zeros((span, HEAD_DIM), jnp.float32)
    for r in range(ratio):
        sl = slice(r * HEAD_DIM, (r + 1) * HEAD_DIM)
        q = q_ref[:, sl]
        dout = do_ref[:, sl]
        out = o_ref[:, sl]
        s = lax.dot_general(q, keys, by_cols, preferred_element_type=jnp.float32) * scale
        s = jnp.where(linked, s, -jnp.inf)
        peak = jnp.max(s, axis=1, keepdims=True)
        raised = jnp.exp(s - peak)
        probs = raised / jnp.sum(raised, axis=1, keepdims=True)
        dp = lax.dot_general(dout, values, by_cols, preferred_element_type=jnp.float32)
        delta = jnp.sum(dout.astype(jnp.float32) * out.astype(jnp.float32), axis=1, keepdims=True)
        ds = (probs * (dp - delta)).astype(jnp.bfloat16)
        dq = jnp.dot(ds, keys, preferred_element_type=jnp.float32) * scale
        dq_ref[:, sl] = dq.astype(dq_ref.dtype)
        dk = dk + lax.dot_general(ds, q, by_rows, preferred_element_type=jnp.float32)
        dv = dv + lax.dot_general(
            probs.astype(jnp.bfloat16), dout, by_rows, preferred_element_type=jnp.float32
        )
    dk_ref[0] = dk * scale
    dv_ref[0] = dv


def attention_grads(queries, outputs, douts, ext_keys, ext_values, interpret=False):
    rows, width_all = queries.shape
    span, kv_width = ext_keys.shape
    groups = kv_width // HEAD_DIM
    width = width_all // groups
    keys4 = ext_keys.reshape(span, groups, HEAD_DIM).transpose(1, 0, 2)
    values4 = ext_values.reshape(span, groups, HEAD_DIM).transpose(1, 0, 2)
    row_block = pl.BlockSpec((rows, width), lambda c: (0, c))
    kv_block = pl.BlockSpec((1, span, HEAD_DIM), lambda c: (c, 0, 0))
    dq, dk4, dv4 = pl.pallas_call(
        attn_kernel,
        grid=(groups,),
        in_specs=[row_block, row_block, row_block, kv_block, kv_block],
        out_specs=[row_block, kv_block, kv_block],
        out_shape=[
            jax.ShapeDtypeStruct((rows, width_all), jnp.bfloat16),
            jax.ShapeDtypeStruct((groups, span, HEAD_DIM), jnp.float32),
            jax.ShapeDtypeStruct((groups, span, HEAD_DIM), jnp.float32),
        ],
        interpret=interpret,
    )(queries, outputs, douts, keys4, values4)
    key_acc = dk4.transpose(1, 0, 2).reshape(span, kv_width)
    value_acc = dv4.transpose(1, 0, 2).reshape(span, kv_width)
    return dq, key_acc, value_acc


def body(
    layer_input,
    query_rows,
    key_rows,
    value_rows,
    saved_output,
    output_grad,
    weight_query,
    weight_key,
    weight_value,
):
    inputs = layer_input[0]
    queries = query_rows[0]
    keys_own = key_rows[0]
    values_own = value_rows[0]
    outputs_own = saved_output[0]
    douts = output_grad[0]
    tokens = queries.shape[0]
    kv_width = keys_own.shape[1]
    width = HEADS // KV_HEADS * HEAD_DIM
    block = min(512, tokens)
    tail_pair = jnp.stack([keys_own, values_own])
    prior_pair = shifted(tail_pair, "seq", 1)
    prior_inputs = shifted(inputs, "seq", 1)
    ext_keys = jnp.concatenate([prior_pair[0], keys_own], axis=0)
    ext_values = jnp.concatenate([prior_pair[1], values_own], axis=0)
    query_blocks, key_acc, value_acc = attention_grads(
        queries[0:block], outputs_own[0:block], douts[0:block],
        ext_keys[0 : block + WINDOW], ext_values[0 : block + WINDOW],
    )
    front_pair = jnp.stack([key_acc[:WINDOW], value_acc[:WINDOW]])
    returned = shifted(front_pair, "seq", -1)
    key_grad = key_acc[WINDOW:].at[tokens - WINDOW :].add(returned[0]).astype(jnp.bfloat16)
    value_grad = value_acc[WINDOW:].at[tokens - WINDOW :].add(returned[1]).astype(jnp.bfloat16)
    contract_cols = (((1,), (1,)), ((), ()))
    summed = lax.dot_general(
        query_blocks, weight_query, contract_cols, preferred_element_type=jnp.float32
    )
    summed = summed + lax.dot_general(
        key_grad, weight_key, contract_cols, preferred_element_type=jnp.float32
    )
    summed = summed + lax.dot_general(
        value_grad, weight_value, contract_cols, preferred_element_type=jnp.float32
    )
    input_grad = summed.astype(jnp.bfloat16)[None]
    own_grads = jnp.concatenate(
        [query_blocks, key_acc[WINDOW:].astype(jnp.bfloat16), value_acc[WINDOW:].astype(jnp.bfloat16)],
        axis=1,
    )
    front_grads = jnp.concatenate(
        [key_acc[:WINDOW].astype(jnp.bfloat16), value_acc[:WINDOW].astype(jnp.bfloat16)], axis=1
    )
    by_tokens = (((0,), (0,)), ((), ()))
    partial = lax.dot_general(inputs, own_grads, by_tokens, preferred_element_type=jnp.float32)
    front_part = lax.dot_general(
        prior_inputs[tokens - WINDOW :], front_grads, by_tokens, preferred_element_type=jnp.float32
    )
    q_span = query_blocks.shape[1]
    partial = partial.at[:, q_span:].add(front_part)
    owned = lax.psum_scatter(partial, ("seq", "lat"), scatter_dimension=0, tiled=True)
    q_width = HEADS * HEAD_DIM
    query_weight_grad = owned[:, :q_width]
    key_weight_grad = owned[:, q_width : q_width + kv_width]
    value_weight_grad = owned[:, q_width + kv_width :]
    return (input_grad, query_weight_grad, key_weight_grad, value_weight_grad)


def solution(mesh):
    placed = (
        P(("parts", "lat"), "seq", None),
        P(("parts", "lat"), "seq", None),
        P(("parts", "lat"), "seq", None),
        P(("parts", "lat"), "seq", None),
        P(("parts", "lat"), "seq", None),
        P(("parts", "lat"), "seq", None),
        P(),
        P(),
        P(),
    )
    return jax.shard_map(
        body,
        mesh=mesh,
        in_specs=placed,
        out_specs=(
            P(("parts", "lat"), "seq", None),
            P(("parts", "seq", "lat"), None),
            P(("parts", "seq", "lat"), None),
            P(("parts", "seq", "lat"), None),
        ),
        check_vma=False,
    )
```

```python
import jax
import jax.numpy as jnp
from jax import lax
from jax.experimental import pallas as pl
from jax.experimental.pallas import tpu as pltpu
from jax.sharding import PartitionSpec as P

HEADS = 16
HEAD_DIM = 64
KV_HEADS = 4
WINDOW = 512
ROW_BLOCK = 256


def shifted(block, axis, distance):
    devices = range(lax.axis_size(axis))
    route = [((i - distance) % len(devices), i) for i in devices]
    return lax.ppermute(block, axis, route)


def attn_kernel(q_ref, o_ref, do_ref, k_ref, v_ref, own_ref, front_ref, own32_ref, front32_ref,
                dk_scr, dv_scr):
    rows = q_ref.shape[0]
    ratio = HEADS // KV_HEADS
    scale = HEAD_DIM ** (-0.5)
    span = ROW_BLOCK + WINDOW
    q_width = HEADS * HEAD_DIM
    kv_width = KV_HEADS * HEAD_DIM
    row = lax.broadcasted_iota(jnp.int32, (ROW_BLOCK, span), 0)
    col = lax.broadcasted_iota(jnp.int32, (ROW_BLOCK, span), 1)
    linked = (col > row) & (col <= row + WINDOW)
    by_rows = (((0,), (0,)), ((), ()))
    by_cols = (((1,), (1,)), ((), ()))
    for c in range(KV_HEADS):
        kv_cols = slice(c * HEAD_DIM, (c + 1) * HEAD_DIM)
        dk_scr[...] = jnp.zeros(dk_scr.shape, jnp.float32)
        dv_scr[...] = jnp.zeros(dv_scr.shape, jnp.float32)

        def row_step(a, carry):
            top = a * ROW_BLOCK
            keys = k_ref[c, pl.ds(top, span), :]
            values = v_ref[c, pl.ds(top, span), :]
            dk = jnp.zeros((HEAD_DIM, span), jnp.float32)
            dv = jnp.zeros((HEAD_DIM, span), jnp.float32)
            for r in range(ratio):
                sl = slice((c * ratio + r) * HEAD_DIM, (c * ratio + r + 1) * HEAD_DIM)
                q = q_ref[pl.ds(top, ROW_BLOCK), sl]
                q_scaled = q * jnp.asarray(scale, q.dtype)
                dout = do_ref[pl.ds(top, ROW_BLOCK), sl]
                out = o_ref[pl.ds(top, ROW_BLOCK), sl]
                s = lax.dot_general(q_scaled, keys, by_cols, preferred_element_type=jnp.float32)
                s = jnp.where(linked, s, -jnp.inf)
                peak = jnp.max(s, axis=1, keepdims=True)
                raised = jnp.exp(s - peak)
                probs = raised * (1.0 / jnp.sum(raised, axis=1, keepdims=True))
                dp = lax.dot_general(dout, values, by_cols, preferred_element_type=jnp.float32)
                delta = jnp.sum(
                    dout.astype(jnp.float32) * out.astype(jnp.float32), axis=1, keepdims=True
                )
                ds = (probs * (dp - delta)).astype(jnp.bfloat16)
                dq = jnp.dot(ds, keys, preferred_element_type=jnp.float32) * scale
                own_ref[pl.ds(top, ROW_BLOCK), sl] = dq.astype(own_ref.dtype)
                dk = dk + lax.dot_general(q, ds, by_rows, preferred_element_type=jnp.float32)
                dv = dv + lax.dot_general(
                    dout, probs.astype(jnp.bfloat16), by_rows, preferred_element_type=jnp.float32
                )
            dk_scr[:, top : top + span] += dk
            dv_scr[:, top : top + span] += dv
            return carry

        for a in range(rows // ROW_BLOCK):
            row_step(a, 0)
        dk_all = dk_scr[...].T * scale
        dv_all = dv_scr[...].T
        k_cols = slice(q_width + c * HEAD_DIM, q_width + (c + 1) * HEAD_DIM)
        v_cols = slice(q_width + kv_width + c * HEAD_DIM, q_width + kv_width + (c + 1) * HEAD_DIM)
        own_ref[:, k_cols] = dk_all[WINDOW:].astype(own_ref.dtype)
        own_ref[:, v_cols] = dv_all[WINDOW:].astype(own_ref.dtype)
        front_ref[:, kv_cols] = dk_all[:WINDOW].astype(front_ref.dtype)
        front_ref[:, slice(kv_width + c * HEAD_DIM, kv_width + (c + 1) * HEAD_DIM)] = (
            dv_all[:WINDOW].astype(front_ref.dtype)
        )
        own32_ref[0, :, kv_cols] = dk_all[WINDOW:]
        own32_ref[1, :, kv_cols] = dv_all[WINDOW:]
        front32_ref[0, :, kv_cols] = dk_all[:WINDOW]
        front32_ref[1, :, kv_cols] = dv_all[:WINDOW]


def attention_grads(queries, outputs, douts, ext_keys, ext_values):
    rows, q_width = queries.shape
    span, kv_width = ext_keys.shape
    ext_keys = ext_keys.reshape(span, KV_HEADS, HEAD_DIM).transpose(1, 0, 2)
    ext_values = ext_values.reshape(span, KV_HEADS, HEAD_DIM).transpose(1, 0, 2)
    vmem = pltpu.MemorySpace.VMEM if hasattr(pltpu, "MemorySpace") else pltpu.VMEM
    return pl.pallas_call(
        attn_kernel,
        out_shape=[
            jax.ShapeDtypeStruct((rows, q_width + 2 * kv_width), jnp.bfloat16),
            jax.ShapeDtypeStruct((span - rows, 2 * kv_width), jnp.bfloat16),
            jax.ShapeDtypeStruct((2, rows, kv_width), jnp.float32),
            jax.ShapeDtypeStruct((2, span - rows, kv_width), jnp.float32),
        ],
        scratch_shapes=[
            pltpu.VMEM((HEAD_DIM, span), jnp.float32),
            pltpu.VMEM((HEAD_DIM, span), jnp.float32),
        ],
    )(queries, outputs, douts, ext_keys, ext_values)


def body(
    layer_input,
    query_rows,
    key_rows,
    value_rows,
    saved_output,
    output_grad,
    weight_query,
    weight_key,
    weight_value,
):
    inputs = layer_input[0]
    queries = query_rows[0]
    keys_own = key_rows[0]
    values_own = value_rows[0]
    outputs_own = saved_output[0]
    douts = output_grad[0]
    tokens = queries.shape[0]
    kv_width = keys_own.shape[1]
    width = HEADS // KV_HEADS * HEAD_DIM
    block = min(512, tokens)
    prior_keys = shifted(keys_own, "seq", 1)
    prior_values = shifted(values_own, "seq", 1)
    prior_inputs = shifted(inputs, "seq", 1)
    ext_keys = jnp.concatenate([prior_keys, keys_own], axis=0)
    ext_values = jnp.concatenate([prior_values, values_own], axis=0)
    own_grads, front_grads, own32, front32 = attention_grads(
        queries, outputs_own, douts, ext_keys, ext_values
    )
    q_span = HEADS * HEAD_DIM
    query_blocks = own_grads[:, :q_span]
    returned = shifted(front32, "seq", -1)
    key_grad = own32[0].at[tokens - WINDOW :].add(returned[0]).astype(jnp.bfloat16)
    value_grad = own32[1].at[tokens - WINDOW :].add(returned[1]).astype(jnp.bfloat16)
    contract_cols = (((1,), (1,)), ((), ()))
    summed = lax.dot_general(
        query_blocks, weight_query, contract_cols, preferred_element_type=jnp.float32
    )
    summed = summed + lax.dot_general(
        key_grad, weight_key, contract_cols, preferred_element_type=jnp.float32
    )
    summed = summed + lax.dot_general(
        value_grad, weight_value, contract_cols, preferred_element_type=jnp.float32
    )
    input_grad = summed.astype(jnp.bfloat16)[None]
    by_tokens = (((0,), (0,)), ((), ()))
    partial = lax.dot_general(inputs, own_grads, by_tokens, preferred_element_type=jnp.float32)
    front_part = lax.dot_general(
        prior_inputs[tokens - WINDOW :], front_grads, by_tokens, preferred_element_type=jnp.float32
    )
    partial = partial.at[:, q_span:].add(front_part)
    owned = lax.psum_scatter(partial, ("seq", "lat"), scatter_dimension=0, tiled=True)
    q_width = HEADS * HEAD_DIM
    query_weight_grad = owned[:, :q_width]
    key_weight_grad = owned[:, q_width : q_width + kv_width]
    value_weight_grad = owned[:, q_width + kv_width :]
    return (input_grad, query_weight_grad, key_weight_grad, value_weight_grad)


def solution(mesh):
    placed = (
        P(("parts", "lat"), "seq", None),
        P(("parts", "lat"), "seq", None),
        P(("parts", "lat"), "seq", None),
        P(("parts", "lat"), "seq", None),
        P(("parts", "lat"), "seq", None),
        P(("parts", "lat"), "seq", None),
        P(),
        P(),
        P(),
    )
    return jax.shard_map(
        body,
        mesh=mesh,
        in_specs=placed,
        out_specs=(
            P(("parts", "lat"), "seq", None),
            P(("parts", "seq", "lat"), None),
            P(("parts", "seq", "lat"), None),
            P(("parts", "seq", "lat"), None),
        ),
        check_vma=False,
    )
```

```python
import jax
import jax.numpy as jnp
from jax import lax
from jax.experimental import pallas as pl
from jax.experimental.pallas import tpu as pltpu
from jax.sharding import PartitionSpec as P

HEADS = 16
HEAD_DIM = 64
KV_HEADS = 4
WINDOW = 512
ROW_BLOCK = 256


def shifted(block, axis, distance):
    devices = range(lax.axis_size(axis))
    route = [((i - distance) % len(devices), i) for i in devices]
    return lax.ppermute(block, axis, route)


def attn_kernel(q_ref, o_ref, do_ref, k_ref, v_ref, own_ref, front_ref, own32_ref, front32_ref,
                dk_scr, dv_scr):
    rows = q_ref.shape[0]
    ratio = HEADS // KV_HEADS
    scale = HEAD_DIM ** (-0.5)
    span = ROW_BLOCK + WINDOW
    q_width = HEADS * HEAD_DIM
    kv_width = KV_HEADS * HEAD_DIM
    row = lax.broadcasted_iota(jnp.int32, (ROW_BLOCK, span), 0)
    col = lax.broadcasted_iota(jnp.int32, (ROW_BLOCK, span), 1)
    linked = (col > row) & (col <= row + WINDOW)
    by_rows = (((0,), (0,)), ((), ()))
    by_cols = (((1,), (1,)), ((), ()))
    for c in range(KV_HEADS):
        kv_cols = slice(c * HEAD_DIM, (c + 1) * HEAD_DIM)
        dk_scr[...] = jnp.zeros(dk_scr.shape, jnp.float32)
        dv_scr[...] = jnp.zeros(dv_scr.shape, jnp.float32)

        def row_step(a, carry):
            top = a * ROW_BLOCK
            keys = k_ref[top : top + span, kv_cols]
            values = v_ref[top : top + span, kv_cols]
            dk = jnp.zeros((HEAD_DIM, span), jnp.float32)
            dv = jnp.zeros((HEAD_DIM, span), jnp.float32)
            for r in range(ratio):
                sl = slice((c * ratio + r) * HEAD_DIM, (c * ratio + r + 1) * HEAD_DIM)
                q = q_ref[pl.ds(top, ROW_BLOCK), sl]
                q_scaled = q * jnp.asarray(scale, q.dtype)
                dout = do_ref[pl.ds(top, ROW_BLOCK), sl]
                out = o_ref[pl.ds(top, ROW_BLOCK), sl]
                s = lax.dot_general(q_scaled, keys, by_cols, preferred_element_type=jnp.float32)
                s = jnp.where(linked, s, -jnp.inf)
                peak = jnp.max(s, axis=1, keepdims=True)
                raised = jnp.exp(s - peak)
                probs = raised * (1.0 / jnp.sum(raised, axis=1, keepdims=True))
                dp = lax.dot_general(dout, values, by_cols, preferred_element_type=jnp.float32)
                delta = jnp.sum(
                    dout.astype(jnp.float32) * out.astype(jnp.float32), axis=1, keepdims=True
                )
                ds = (probs * (dp - delta)).astype(jnp.bfloat16)
                dq = jnp.dot(ds, keys, preferred_element_type=jnp.float32) * scale
                own_ref[pl.ds(top, ROW_BLOCK), sl] = dq.astype(own_ref.dtype)
                dk = dk + lax.dot_general(q, ds, by_rows, preferred_element_type=jnp.float32)
                dv = dv + lax.dot_general(
                    dout, probs.astype(jnp.bfloat16), by_rows, preferred_element_type=jnp.float32
                )
            dk_scr[:, top : top + span] += dk
            dv_scr[:, top : top + span] += dv
            return carry

        for a in range(rows // ROW_BLOCK):
            row_step(a, 0)
        dk_all = dk_scr[...].T * scale
        dv_all = dv_scr[...].T
        k_cols = slice(q_width + c * HEAD_DIM, q_width + (c + 1) * HEAD_DIM)
        v_cols = slice(q_width + kv_width + c * HEAD_DIM, q_width + kv_width + (c + 1) * HEAD_DIM)
        own_ref[:, k_cols] = dk_all[WINDOW:].astype(own_ref.dtype)
        own_ref[:, v_cols] = dv_all[WINDOW:].astype(own_ref.dtype)
        front_ref[:, kv_cols] = dk_all[:WINDOW].astype(front_ref.dtype)
        front_ref[:, slice(kv_width + c * HEAD_DIM, kv_width + (c + 1) * HEAD_DIM)] = (
            dv_all[:WINDOW].astype(front_ref.dtype)
        )
        own32_ref[0, :, kv_cols] = dk_all[WINDOW:]
        own32_ref[1, :, kv_cols] = dv_all[WINDOW:]
        front32_ref[0, :, kv_cols] = dk_all[:WINDOW]
        front32_ref[1, :, kv_cols] = dv_all[:WINDOW]


def attention_grads(queries, outputs, douts, ext_keys, ext_values):
    rows, q_width = queries.shape
    span, kv_width = ext_keys.shape
    vmem = pltpu.MemorySpace.VMEM if hasattr(pltpu, "MemorySpace") else pltpu.VMEM
    return pl.pallas_call(
        attn_kernel,
        out_shape=[
            jax.ShapeDtypeStruct((rows, q_width + 2 * kv_width), jnp.bfloat16),
            jax.ShapeDtypeStruct((span - rows, 2 * kv_width), jnp.bfloat16),
            jax.ShapeDtypeStruct((2, rows, kv_width), jnp.float32),
            jax.ShapeDtypeStruct((2, span - rows, kv_width), jnp.float32),
        ],
        scratch_shapes=[
            pltpu.VMEM((HEAD_DIM, span), jnp.float32),
            pltpu.VMEM((HEAD_DIM, span), jnp.float32),
        ],
    )(queries, outputs, douts, ext_keys, ext_values)


def wgrad_kernel(x_ref, xp_ref, own_ref, front_ref, out_ref):
    by_rows = (((0,), (0,)), ((), ()))
    q_width = out_ref.shape[1] - front_ref.shape[1]
    own_part = lax.dot_general(x_ref[...], own_ref[...], by_rows, preferred_element_type=jnp.float32)
    front_part = lax.dot_general(
        xp_ref[...], front_ref[...], by_rows, preferred_element_type=jnp.float32
    )
    out_ref[:, :q_width] = own_part[:, :q_width]
    out_ref[:, q_width:] = own_part[:, q_width:] + front_part


def weight_partial(inputs, prior_inputs, own_grads, front_grads):
    tokens, model = inputs.shape
    width = own_grads.shape[1]
    cols = 256 if model % 256 == 0 else model
    x_block = pl.BlockSpec((tokens, cols), lambda i: (0, i))
    return pl.pallas_call(
        wgrad_kernel,
        grid=(model // cols,),
        in_specs=[
            x_block,
            x_block,
            pl.BlockSpec(own_grads.shape, lambda i: (0, 0)),
            pl.BlockSpec(front_grads.shape, lambda i: (0, 0)),
        ],
        out_specs=pl.BlockSpec((cols, width), lambda i: (i, 0)),
        out_shape=jax.ShapeDtypeStruct((model, width), jnp.float32),
    )(inputs, prior_inputs, own_grads, front_grads)


def body(
    layer_input,
    query_rows,
    key_rows,
    value_rows,
    saved_output,
    output_grad,
    weight_query,
    weight_key,
    weight_value,
):
    inputs = layer_input[0]
    queries = query_rows[0]
    keys_own = key_rows[0]
    values_own = value_rows[0]
    outputs_own = saved_output[0]
    douts = output_grad[0]
    tokens = queries.shape[0]
    kv_width = keys_own.shape[1]
    prior_keys = shifted(keys_own, "seq", 1)
    prior_values = shifted(values_own, "seq", 1)
    inputs_after, prior_keys, prior_values = lax.optimization_barrier(
        (inputs, prior_keys, prior_values)
    )
    prior_inputs = shifted(inputs_after, "seq", 1)
    ext_keys = jnp.concatenate([prior_keys, keys_own], axis=0)
    ext_values = jnp.concatenate([prior_values, values_own], axis=0)
    own_grads, front_grads, own32, front32 = attention_grads(
        queries, outputs_own, douts, ext_keys, ext_values
    )
    q_span = HEADS * HEAD_DIM
    query_blocks = own_grads[:, :q_span]
    returned = shifted(front32, "seq", -1)
    key_grad = own32[0].at[tokens - WINDOW :].add(returned[0]).astype(jnp.bfloat16)
    value_grad = own32[1].at[tokens - WINDOW :].add(returned[1]).astype(jnp.bfloat16)
    contract_cols = (((1,), (1,)), ((), ()))
    summed = lax.dot_general(
        query_blocks, weight_query, contract_cols, preferred_element_type=jnp.float32
    )
    summed = summed + lax.dot_general(
        key_grad, weight_key, contract_cols, preferred_element_type=jnp.float32
    )
    summed = summed + lax.dot_general(
        value_grad, weight_value, contract_cols, preferred_element_type=jnp.float32
    )
    input_grad = summed.astype(jnp.bfloat16)[None]
    partial = weight_partial(inputs, prior_inputs[tokens - WINDOW :], own_grads, front_grads)
    owned = lax.psum_scatter(partial, ("seq", "lat"), scatter_dimension=0, tiled=True)
    q_width = HEADS * HEAD_DIM
    query_weight_grad = owned[:, :q_width]
    key_weight_grad = owned[:, q_width : q_width + kv_width]
    value_weight_grad = owned[:, q_width + kv_width :]
    return (input_grad, query_weight_grad, key_weight_grad, value_weight_grad)


def solution(mesh):
    placed = (
        P(("parts", "lat"), "seq", None),
        P(("parts", "lat"), "seq", None),
        P(("parts", "lat"), "seq", None),
        P(("parts", "lat"), "seq", None),
        P(("parts", "lat"), "seq", None),
        P(("parts", "lat"), "seq", None),
        P(),
        P(),
        P(),
    )
    return jax.shard_map(
        body,
        mesh=mesh,
        in_specs=placed,
        out_specs=(
            P(("parts", "lat"), "seq", None),
            P(("parts", "seq", "lat"), None),
            P(("parts", "seq", "lat"), None),
            P(("parts", "seq", "lat"), None),
        ),
        check_vma=False,
    )
```

```python
import jax
import jax.numpy as jnp
from jax import lax
from jax.experimental import pallas as pl
from jax.experimental.pallas import tpu as pltpu
from jax.sharding import PartitionSpec as P

HEADS = 16
HEAD_DIM = 64
KV_HEADS = 4
WINDOW = 512
ROW_BLOCK = 256


def shifted(block, axis, distance):
    devices = range(lax.axis_size(axis))
    route = [((i - distance) % len(devices), i) for i in devices]
    return lax.ppermute(block, axis, route)


def attn_kernel(q_ref, o_ref, do_ref, k_ref, v_ref, own_ref, front_ref, own32_ref, front32_ref,
                dk_scr, dv_scr):
    rows = q_ref.shape[0]
    ratio = HEADS // KV_HEADS
    scale = HEAD_DIM ** (-0.5)
    span = ROW_BLOCK + WINDOW
    q_width = HEADS * HEAD_DIM
    kv_width = KV_HEADS * HEAD_DIM
    stacked = ratio * ROW_BLOCK
    row = lax.broadcasted_iota(jnp.int32, (stacked, span), 0) % ROW_BLOCK
    col = lax.broadcasted_iota(jnp.int32, (stacked, span), 1)
    linked = (col > row) & (col <= row + WINDOW)
    by_rows = (((0,), (0,)), ((), ()))
    by_cols = (((1,), (1,)), ((), ()))
    for c in range(KV_HEADS):
        kv_cols = slice(c * HEAD_DIM, (c + 1) * HEAD_DIM)
        dk_scr[...] = jnp.zeros(dk_scr.shape, jnp.float32)
        dv_scr[...] = jnp.zeros(dv_scr.shape, jnp.float32)
        for a in range(rows // ROW_BLOCK):
            top = a * ROW_BLOCK
            keys = k_ref[top : top + span, kv_cols]
            values = v_ref[top : top + span, kv_cols]
            heads = [slice((c * ratio + r) * HEAD_DIM, (c * ratio + r + 1) * HEAD_DIM) for r in range(ratio)]
            q = jnp.concatenate([q_ref[top : top + ROW_BLOCK, sl] for sl in heads], axis=0)
            dout = jnp.concatenate([do_ref[top : top + ROW_BLOCK, sl] for sl in heads], axis=0)
            out = jnp.concatenate([o_ref[top : top + ROW_BLOCK, sl] for sl in heads], axis=0)
            q_scaled = q * jnp.asarray(scale, q.dtype)
            s = lax.dot_general(q_scaled, keys, by_cols, preferred_element_type=jnp.float32)
            s = jnp.where(linked, s, -jnp.inf)
            peak = jnp.max(s, axis=1, keepdims=True)
            raised = jnp.exp(s - peak)
            probs = raised * (1.0 / jnp.sum(raised, axis=1, keepdims=True))
            dp = lax.dot_general(dout, values, by_cols, preferred_element_type=jnp.float32)
            delta = jnp.sum(dout.astype(jnp.float32) * out.astype(jnp.float32), axis=1, keepdims=True)
            ds = (probs * (dp - delta)).astype(jnp.bfloat16)
            dq = jnp.dot(ds, keys, preferred_element_type=jnp.float32) * scale
            for r, sl in enumerate(heads):
                own_ref[top : top + ROW_BLOCK, sl] = dq[r * ROW_BLOCK : (r + 1) * ROW_BLOCK].astype(own_ref.dtype)
            dk_scr[:, top : top + span] += lax.dot_general(q, ds, by_rows, preferred_element_type=jnp.float32)
            dv_scr[:, top : top + span] += lax.dot_general(
                dout, probs.astype(jnp.bfloat16), by_rows, preferred_element_type=jnp.float32
            )
        dk_all = dk_scr[...].T * scale
        dv_all = dv_scr[...].T
        k_cols = slice(q_width + c * HEAD_DIM, q_width + (c + 1) * HEAD_DIM)
        v_cols = slice(q_width + kv_width + c * HEAD_DIM, q_width + kv_width + (c + 1) * HEAD_DIM)
        own_ref[:, k_cols] = dk_all[WINDOW:].astype(own_ref.dtype)
        own_ref[:, v_cols] = dv_all[WINDOW:].astype(own_ref.dtype)
        front_ref[:, kv_cols] = dk_all[:WINDOW].astype(front_ref.dtype)
        front_ref[:, slice(kv_width + c * HEAD_DIM, kv_width + (c + 1) * HEAD_DIM)] = (
            dv_all[:WINDOW].astype(front_ref.dtype)
        )
        own32_ref[0, :, kv_cols] = dk_all[WINDOW:]
        own32_ref[1, :, kv_cols] = dv_all[WINDOW:]
        front32_ref[0, :, kv_cols] = dk_all[:WINDOW]
        front32_ref[1, :, kv_cols] = dv_all[:WINDOW]


def attention_grads(queries, outputs, douts, ext_keys, ext_values):
    rows, q_width = queries.shape
    span, kv_width = ext_keys.shape
    vmem = pltpu.MemorySpace.VMEM if hasattr(pltpu, "MemorySpace") else pltpu.VMEM
    return pl.pallas_call(
        attn_kernel,
        out_shape=[
            jax.ShapeDtypeStruct((rows, q_width + 2 * kv_width), jnp.bfloat16),
            jax.ShapeDtypeStruct((span - rows, 2 * kv_width), jnp.bfloat16),
            jax.ShapeDtypeStruct((2, rows, kv_width), jnp.float32),
            jax.ShapeDtypeStruct((2, span - rows, kv_width), jnp.float32),
        ],
        scratch_shapes=[
            pltpu.VMEM((HEAD_DIM, span), jnp.float32),
            pltpu.VMEM((HEAD_DIM, span), jnp.float32),
        ],
    )(queries, outputs, douts, ext_keys, ext_values)


def wgrad_kernel(x_ref, xp_ref, own_ref, front_ref, out_ref):
    by_rows = (((0,), (0,)), ((), ()))
    q_width = out_ref.shape[1] - front_ref.shape[1]
    own_part = lax.dot_general(x_ref[...], own_ref[...], by_rows, preferred_element_type=jnp.float32)
    front_part = lax.dot_general(
        xp_ref[...], front_ref[...], by_rows, preferred_element_type=jnp.float32
    )
    out_ref[:, :q_width] = own_part[:, :q_width]
    out_ref[:, q_width:] = own_part[:, q_width:] + front_part


def weight_partial(inputs, prior_inputs, own_grads, front_grads):
    tokens, model = inputs.shape
    width = own_grads.shape[1]
    cols = 256 if model % 256 == 0 else model
    x_block = pl.BlockSpec((tokens, cols), lambda i: (0, i))
    return pl.pallas_call(
        wgrad_kernel,
        grid=(model // cols,),
        in_specs=[
            x_block,
            x_block,
            pl.BlockSpec(own_grads.shape, lambda i: (0, 0)),
            pl.BlockSpec(front_grads.shape, lambda i: (0, 0)),
        ],
        out_specs=pl.BlockSpec((cols, width), lambda i: (i, 0)),
        out_shape=jax.ShapeDtypeStruct((model, width), jnp.float32),
    )(inputs, prior_inputs, own_grads, front_grads)


def body(
    layer_input,
    query_rows,
    key_rows,
    value_rows,
    saved_output,
    output_grad,
    weight_query,
    weight_key,
    weight_value,
):
    inputs = layer_input[0]
    queries = query_rows[0]
    keys_own = key_rows[0]
    values_own = value_rows[0]
    outputs_own = saved_output[0]
    douts = output_grad[0]
    tokens = queries.shape[0]
    kv_width = keys_own.shape[1]
    prior_keys = shifted(keys_own, "seq", 1)
    prior_values = shifted(values_own, "seq", 1)
    inputs_after, prior_keys, prior_values = lax.optimization_barrier(
        (inputs, prior_keys, prior_values)
    )
    prior_inputs = shifted(inputs_after, "seq", 1)
    ext_keys = jnp.concatenate([prior_keys, keys_own], axis=0)
    ext_values = jnp.concatenate([prior_values, values_own], axis=0)
    own_grads, front_grads, own32, front32 = attention_grads(
        queries, outputs_own, douts, ext_keys, ext_values
    )
    q_span = HEADS * HEAD_DIM
    query_blocks = own_grads[:, :q_span]
    returned = shifted(front32, "seq", -1)
    key_grad = own32[0].at[tokens - WINDOW :].add(returned[0]).astype(jnp.bfloat16)
    value_grad = own32[1].at[tokens - WINDOW :].add(returned[1]).astype(jnp.bfloat16)
    contract_cols = (((1,), (1,)), ((), ()))
    summed = lax.dot_general(
        query_blocks, weight_query, contract_cols, preferred_element_type=jnp.float32
    )
    summed = summed + lax.dot_general(
        key_grad, weight_key, contract_cols, preferred_element_type=jnp.float32
    )
    summed = summed + lax.dot_general(
        value_grad, weight_value, contract_cols, preferred_element_type=jnp.float32
    )
    input_grad = summed.astype(jnp.bfloat16)[None]
    partial = weight_partial(inputs, prior_inputs[tokens - WINDOW :], own_grads, front_grads)
    owned = lax.psum_scatter(partial, ("seq", "lat"), scatter_dimension=0, tiled=True)
    q_width = HEADS * HEAD_DIM
    query_weight_grad = owned[:, :q_width]
    key_weight_grad = owned[:, q_width : q_width + kv_width]
    value_weight_grad = owned[:, q_width + kv_width :]
    return (input_grad, query_weight_grad, key_weight_grad, value_weight_grad)


def solution(mesh):
    placed = (
        P(("parts", "lat"), "seq", None),
        P(("parts", "lat"), "seq", None),
        P(("parts", "lat"), "seq", None),
        P(("parts", "lat"), "seq", None),
        P(("parts", "lat"), "seq", None),
        P(("parts", "lat"), "seq", None),
        P(),
        P(),
        P(),
    )
    return jax.shard_map(
        body,
        mesh=mesh,
        in_specs=placed,
        out_specs=(
            P(("parts", "lat"), "seq", None),
            P(("parts", "seq", "lat"), None),
            P(("parts", "seq", "lat"), None),
            P(("parts", "seq", "lat"), None),
        ),
        check_vma=False,
    )
```

```python
import jax
import jax.numpy as jnp
from jax import lax
from jax.experimental import pallas as pl
from jax.experimental.pallas import tpu as pltpu
from jax.sharding import PartitionSpec as P

HEADS = 16
HEAD_DIM = 64
KV_HEADS = 4
WINDOW = 512
ROW_BLOCK = 256


def shifted(block, axis, distance):
    devices = range(lax.axis_size(axis))
    route = [((i - distance) % len(devices), i) for i in devices]
    return lax.ppermute(block, axis, route)


def attn_kernel(q_ref, o_ref, do_ref, k_ref, v_ref, own_ref, front_ref, own32_ref, front32_ref,
                dk_scr, dv_scr):
    rows = q_ref.shape[0]
    ratio = HEADS // KV_HEADS
    scale = HEAD_DIM ** (-0.5)
    span = ROW_BLOCK + WINDOW
    q_width = HEADS * HEAD_DIM
    kv_width = KV_HEADS * HEAD_DIM
    stacked = ratio * ROW_BLOCK
    row = lax.broadcasted_iota(jnp.int32, (stacked, span), 0) % ROW_BLOCK
    col = lax.broadcasted_iota(jnp.int32, (stacked, span), 1)
    linked = (col > row) & (col <= row + WINDOW)
    by_rows = (((0,), (0,)), ((), ()))
    by_cols = (((1,), (1,)), ((), ()))
    for c in range(KV_HEADS):
        kv_cols = slice(c * HEAD_DIM, (c + 1) * HEAD_DIM)
        dk_scr[...] = jnp.zeros(dk_scr.shape, jnp.float32)
        dv_scr[...] = jnp.zeros(dv_scr.shape, jnp.float32)
        for a in range(rows // ROW_BLOCK):
            top = a * ROW_BLOCK
            keys = k_ref[top : top + span, kv_cols]
            values = v_ref[top : top + span, kv_cols]
            heads = [slice((c * ratio + r) * HEAD_DIM, (c * ratio + r + 1) * HEAD_DIM) for r in range(ratio)]
            q = jnp.concatenate([q_ref[top : top + ROW_BLOCK, sl] for sl in heads], axis=0)
            dout = jnp.concatenate([do_ref[top : top + ROW_BLOCK, sl] for sl in heads], axis=0)
            out = jnp.concatenate([o_ref[top : top + ROW_BLOCK, sl] for sl in heads], axis=0)
            q_scaled = q * jnp.asarray(scale, q.dtype)
            s = lax.dot_general(q_scaled, keys, by_cols, preferred_element_type=jnp.float32)
            s = jnp.where(linked, s, -jnp.inf)
            peak = jnp.max(s, axis=1, keepdims=True)
            raised = jnp.exp(s - peak)
            probs = raised * (1.0 / jnp.sum(raised, axis=1, keepdims=True))
            dp = lax.dot_general(dout, values, by_cols, preferred_element_type=jnp.float32)
            delta = jnp.sum(dout.astype(jnp.float32) * out.astype(jnp.float32), axis=1, keepdims=True)
            ds = (probs * (dp - delta)).astype(jnp.bfloat16)
            dq = jnp.dot(ds, keys, preferred_element_type=jnp.float32) * scale
            for r, sl in enumerate(heads):
                own_ref[top : top + ROW_BLOCK, sl] = dq[r * ROW_BLOCK : (r + 1) * ROW_BLOCK].astype(own_ref.dtype)
            dk_scr[:, top : top + span] += lax.dot_general(q, ds, by_rows, preferred_element_type=jnp.float32)
            dv_scr[:, top : top + span] += lax.dot_general(
                dout, probs.astype(jnp.bfloat16), by_rows, preferred_element_type=jnp.float32
            )
        dk_all = dk_scr[...].T * scale
        dv_all = dv_scr[...].T
        k_cols = slice(q_width + c * HEAD_DIM, q_width + (c + 1) * HEAD_DIM)
        v_cols = slice(q_width + kv_width + c * HEAD_DIM, q_width + kv_width + (c + 1) * HEAD_DIM)
        own_ref[:, k_cols] = dk_all[WINDOW:].astype(own_ref.dtype)
        own_ref[:, v_cols] = dv_all[WINDOW:].astype(own_ref.dtype)
        front_ref[:, kv_cols] = dk_all[:WINDOW].astype(front_ref.dtype)
        front_ref[:, slice(kv_width + c * HEAD_DIM, kv_width + (c + 1) * HEAD_DIM)] = (
            dv_all[:WINDOW].astype(front_ref.dtype)
        )
        own32_ref[0, :, kv_cols] = dk_all[WINDOW:]
        own32_ref[1, :, kv_cols] = dv_all[WINDOW:]
        front32_ref[0, :, kv_cols] = dk_all[:WINDOW]
        front32_ref[1, :, kv_cols] = dv_all[:WINDOW]


def attention_grads(queries, outputs, douts, ext_keys, ext_values):
    rows, q_width = queries.shape
    span, kv_width = ext_keys.shape
    vmem = pltpu.MemorySpace.VMEM if hasattr(pltpu, "MemorySpace") else pltpu.VMEM
    return pl.pallas_call(
        attn_kernel,
        out_shape=[
            jax.ShapeDtypeStruct((rows, q_width + 2 * kv_width), jnp.bfloat16),
            jax.ShapeDtypeStruct((span - rows, 2 * kv_width), jnp.bfloat16),
            jax.ShapeDtypeStruct((2, rows, kv_width), jnp.float32),
            jax.ShapeDtypeStruct((2, span - rows, kv_width), jnp.float32),
        ],
        scratch_shapes=[
            pltpu.VMEM((HEAD_DIM, span), jnp.float32),
            pltpu.VMEM((HEAD_DIM, span), jnp.float32),
        ],
    )(queries, outputs, douts, ext_keys, ext_values)


def wgrad_kernel(x_ref, xp_ref, own_ref, front_ref, out_ref):
    q_width = out_ref.shape[1] - front_ref.shape[1]
    own_part = jnp.dot(x_ref[...], own_ref[...], preferred_element_type=jnp.float32)
    front_part = jnp.dot(xp_ref[...], front_ref[...], preferred_element_type=jnp.float32)
    out_ref[:, :q_width] = own_part[:, :q_width]
    out_ref[:, q_width:] = own_part[:, q_width:] + front_part


def weight_partial(inputs_t, prior_inputs_t, own_grads, front_grads):
    model, tokens = inputs_t.shape
    width = own_grads.shape[1]
    cols = 256 if model % 256 == 0 else model
    x_block = pl.BlockSpec((cols, tokens), lambda i: (i, 0))
    return pl.pallas_call(
        wgrad_kernel,
        grid=(model // cols,),
        in_specs=[
            x_block,
            x_block,
            pl.BlockSpec(own_grads.shape, lambda i: (0, 0)),
            pl.BlockSpec(front_grads.shape, lambda i: (0, 0)),
        ],
        out_specs=pl.BlockSpec((cols, width), lambda i: (i, 0)),
        out_shape=jax.ShapeDtypeStruct((model, width), jnp.float32),
    )(inputs_t, prior_inputs_t, own_grads, front_grads)


def body(
    layer_input,
    query_rows,
    key_rows,
    value_rows,
    saved_output,
    output_grad,
    weight_query,
    weight_key,
    weight_value,
):
    inputs = layer_input[0]
    queries = query_rows[0]
    keys_own = key_rows[0]
    values_own = value_rows[0]
    outputs_own = saved_output[0]
    douts = output_grad[0]
    tokens = queries.shape[0]
    kv_width = keys_own.shape[1]
    prior_keys = shifted(keys_own, "seq", 1)
    prior_values = shifted(values_own, "seq", 1)
    inputs_t = inputs.T
    inputs_after, prior_keys, prior_values = lax.optimization_barrier(
        (inputs_t, prior_keys, prior_values)
    )
    prior_inputs_t = shifted(inputs_after, "seq", 1)
    ext_keys = jnp.concatenate([prior_keys, keys_own], axis=0)
    ext_values = jnp.concatenate([prior_values, values_own], axis=0)
    own_grads, front_grads, own32, front32 = attention_grads(
        queries, outputs_own, douts, ext_keys, ext_values
    )
    q_span = HEADS * HEAD_DIM
    query_blocks = own_grads[:, :q_span]
    returned = shifted(front32, "seq", -1)
    key_grad = own32[0].at[tokens - WINDOW :].add(returned[0]).astype(jnp.bfloat16)
    value_grad = own32[1].at[tokens - WINDOW :].add(returned[1]).astype(jnp.bfloat16)
    contract_cols = (((1,), (1,)), ((), ()))
    summed = lax.dot_general(
        query_blocks, weight_query, contract_cols, preferred_element_type=jnp.float32
    )
    summed = summed + lax.dot_general(
        key_grad, weight_key, contract_cols, preferred_element_type=jnp.float32
    )
    summed = summed + lax.dot_general(
        value_grad, weight_value, contract_cols, preferred_element_type=jnp.float32
    )
    input_grad = summed.astype(jnp.bfloat16)[None]
    partial = weight_partial(inputs_t, prior_inputs_t[:, tokens - WINDOW :], own_grads, front_grads)
    owned = lax.psum_scatter(partial, ("seq", "lat"), scatter_dimension=0, tiled=True)
    q_width = HEADS * HEAD_DIM
    query_weight_grad = owned[:, :q_width]
    key_weight_grad = owned[:, q_width : q_width + kv_width]
    value_weight_grad = owned[:, q_width + kv_width :]
    return (input_grad, query_weight_grad, key_weight_grad, value_weight_grad)


def solution(mesh):
    placed = (
        P(("parts", "lat"), "seq", None),
        P(("parts", "lat"), "seq", None),
        P(("parts", "lat"), "seq", None),
        P(("parts", "lat"), "seq", None),
        P(("parts", "lat"), "seq", None),
        P(("parts", "lat"), "seq", None),
        P(),
        P(),
        P(),
    )
    return jax.shard_map(
        body,
        mesh=mesh,
        in_specs=placed,
        out_specs=(
            P(("parts", "lat"), "seq", None),
            P(("parts", "seq", "lat"), None),
            P(("parts", "seq", "lat"), None),
            P(("parts", "seq", "lat"), None),
        ),
        check_vma=False,
    )
```

```python
import jax
import jax.numpy as jnp
from jax import lax
from jax.experimental import pallas as pl
from jax.experimental.pallas import tpu as pltpu
from jax.sharding import PartitionSpec as P

HEADS = 16
HEAD_DIM = 64
KV_HEADS = 4
WINDOW = 512
ROW_BLOCK = 256


def shifted(block, axis, distance):
    devices = range(lax.axis_size(axis))
    route = [((i - distance) % len(devices), i) for i in devices]
    return lax.ppermute(block, axis, route)


def attn_kernel(q_ref, o_ref, do_ref, kp_ref, ko_ref, vp_ref, vo_ref, own_ref, front_ref,
                own32_ref, front32_ref, dk_scr, dv_scr, k_ref, v_ref):
    prior = kp_ref.shape[0]
    k_ref[:prior, :] = kp_ref[...]
    k_ref[prior:, :] = ko_ref[...]
    v_ref[:prior, :] = vp_ref[...]
    v_ref[prior:, :] = vo_ref[...]
    rows = q_ref.shape[0]
    ratio = HEADS // KV_HEADS
    scale = HEAD_DIM ** (-0.5)
    span = ROW_BLOCK + WINDOW
    q_width = HEADS * HEAD_DIM
    kv_width = KV_HEADS * HEAD_DIM
    stacked = ratio * ROW_BLOCK
    row = lax.broadcasted_iota(jnp.int32, (stacked, span), 0) % ROW_BLOCK
    col = lax.broadcasted_iota(jnp.int32, (stacked, span), 1)
    linked = (col > row) & (col <= row + WINDOW)
    by_rows = (((0,), (0,)), ((), ()))
    by_cols = (((1,), (1,)), ((), ()))
    for c in range(KV_HEADS):
        kv_cols = slice(c * HEAD_DIM, (c + 1) * HEAD_DIM)
        dk_scr[...] = jnp.zeros(dk_scr.shape, jnp.float32)
        dv_scr[...] = jnp.zeros(dv_scr.shape, jnp.float32)
        for a in range(rows // ROW_BLOCK):
            top = a * ROW_BLOCK
            keys = k_ref[top : top + span, kv_cols]
            values = v_ref[top : top + span, kv_cols]
            heads = [slice((c * ratio + r) * HEAD_DIM, (c * ratio + r + 1) * HEAD_DIM) for r in range(ratio)]
            q = jnp.concatenate([q_ref[top : top + ROW_BLOCK, sl] for sl in heads], axis=0)
            dout = jnp.concatenate([do_ref[top : top + ROW_BLOCK, sl] for sl in heads], axis=0)
            out = jnp.concatenate([o_ref[top : top + ROW_BLOCK, sl] for sl in heads], axis=0)
            q_scaled = q * jnp.asarray(scale, q.dtype)
            s = lax.dot_general(q_scaled, keys, by_cols, preferred_element_type=jnp.float32)
            s = jnp.where(linked, s, -jnp.inf)
            peak = jnp.max(s, axis=1, keepdims=True)
            raised = jnp.exp(s - peak)
            probs = raised * (1.0 / jnp.sum(raised, axis=1, keepdims=True))
            dp = lax.dot_general(dout, values, by_cols, preferred_element_type=jnp.float32)
            delta = jnp.sum(dout.astype(jnp.float32) * out.astype(jnp.float32), axis=1, keepdims=True)
            ds = (probs * (dp - delta)).astype(jnp.bfloat16)
            dq = jnp.dot(ds, keys, preferred_element_type=jnp.float32) * scale
            for r, sl in enumerate(heads):
                own_ref[top : top + ROW_BLOCK, sl] = dq[r * ROW_BLOCK : (r + 1) * ROW_BLOCK].astype(own_ref.dtype)
            dk_scr[:, top : top + span] += lax.dot_general(q, ds, by_rows, preferred_element_type=jnp.float32)
            dv_scr[:, top : top + span] += lax.dot_general(
                dout, probs.astype(jnp.bfloat16), by_rows, preferred_element_type=jnp.float32
            )
        dk_all = dk_scr[...].T * scale
        dv_all = dv_scr[...].T
        k_cols = slice(q_width + c * HEAD_DIM, q_width + (c + 1) * HEAD_DIM)
        v_cols = slice(q_width + kv_width + c * HEAD_DIM, q_width + kv_width + (c + 1) * HEAD_DIM)
        own_ref[:, k_cols] = dk_all[WINDOW:].astype(own_ref.dtype)
        own_ref[:, v_cols] = dv_all[WINDOW:].astype(own_ref.dtype)
        front_ref[:, kv_cols] = dk_all[:WINDOW].astype(front_ref.dtype)
        front_ref[:, slice(kv_width + c * HEAD_DIM, kv_width + (c + 1) * HEAD_DIM)] = (
            dv_all[:WINDOW].astype(front_ref.dtype)
        )
        own32_ref[0, :, kv_cols] = dk_all[WINDOW:]
        own32_ref[1, :, kv_cols] = dv_all[WINDOW:]
        front32_ref[0, :, kv_cols] = dk_all[:WINDOW]
        front32_ref[1, :, kv_cols] = dv_all[:WINDOW]


def attention_grads(queries, outputs, douts, prior_keys, keys_own, prior_values, values_own):
    rows, q_width = queries.shape
    prior, kv_width = prior_keys.shape
    span = prior + keys_own.shape[0]
    return pl.pallas_call(
        attn_kernel,
        out_shape=[
            jax.ShapeDtypeStruct((rows, q_width + 2 * kv_width), jnp.bfloat16),
            jax.ShapeDtypeStruct((prior, 2 * kv_width), jnp.bfloat16),
            jax.ShapeDtypeStruct((2, rows, kv_width), jnp.float32),
            jax.ShapeDtypeStruct((2, prior, kv_width), jnp.float32),
        ],
        scratch_shapes=[
            pltpu.VMEM((HEAD_DIM, span), jnp.float32),
            pltpu.VMEM((HEAD_DIM, span), jnp.float32),
            pltpu.VMEM((span, kv_width), prior_keys.dtype),
            pltpu.VMEM((span, kv_width), prior_values.dtype),
        ],
    )(queries, outputs, douts, prior_keys, keys_own, prior_values, values_own)


def wgrad_kernel(x_ref, xp_ref, own_ref, front_ref, out_ref):
    q_width = out_ref.shape[1] - front_ref.shape[1]
    own_part = jnp.dot(x_ref[...], own_ref[...], preferred_element_type=jnp.float32)
    front_part = jnp.dot(xp_ref[...], front_ref[...], preferred_element_type=jnp.float32)
    out_ref[:, :q_width] = own_part[:, :q_width]
    out_ref[:, q_width:] = own_part[:, q_width:] + front_part


def weight_partial(inputs_t, prior_inputs_t, own_grads, front_grads):
    model, tokens = inputs_t.shape
    width = own_grads.shape[1]
    cols = 256 if model % 256 == 0 else model
    x_block = pl.BlockSpec((cols, tokens), lambda i: (i, 0))
    return pl.pallas_call(
        wgrad_kernel,
        grid=(model // cols,),
        in_specs=[
            x_block,
            x_block,
            pl.BlockSpec(own_grads.shape, lambda i: (0, 0)),
            pl.BlockSpec(front_grads.shape, lambda i: (0, 0)),
        ],
        out_specs=pl.BlockSpec((cols, width), lambda i: (i, 0)),
        out_shape=jax.ShapeDtypeStruct((model, width), jnp.float32),
    )(inputs_t, prior_inputs_t, own_grads, front_grads)


def body(
    layer_input,
    query_rows,
    key_rows,
    value_rows,
    saved_output,
    output_grad,
    weight_query,
    weight_key,
    weight_value,
):
    inputs = layer_input[0]
    queries = query_rows[0]
    keys_own = key_rows[0]
    values_own = value_rows[0]
    outputs_own = saved_output[0]
    douts = output_grad[0]
    tokens = queries.shape[0]
    kv_width = keys_own.shape[1]
    prior_keys = shifted(keys_own, "seq", 1)
    prior_values = shifted(values_own, "seq", 1)
    inputs_t = inputs.T
    inputs_after, prior_keys, prior_values = lax.optimization_barrier(
        (inputs_t, prior_keys, prior_values)
    )
    prior_inputs_t = shifted(inputs_after, "seq", 1)
    own_grads, front_grads, own32, front32 = attention_grads(
        queries, outputs_own, douts, prior_keys, keys_own, prior_values, values_own
    )
    q_span = HEADS * HEAD_DIM
    query_blocks = own_grads[:, :q_span]
    returned = shifted(front32, "seq", -1)
    key_grad = own32[0].at[tokens - WINDOW :].add(returned[0]).astype(jnp.bfloat16)
    value_grad = own32[1].at[tokens - WINDOW :].add(returned[1]).astype(jnp.bfloat16)
    contract_cols = (((1,), (1,)), ((), ()))
    summed = lax.dot_general(
        query_blocks, weight_query, contract_cols, preferred_element_type=jnp.float32
    )
    summed = summed + lax.dot_general(
        key_grad, weight_key, contract_cols, preferred_element_type=jnp.float32
    )
    summed = summed + lax.dot_general(
        value_grad, weight_value, contract_cols, preferred_element_type=jnp.float32
    )
    input_grad = summed.astype(jnp.bfloat16)[None]
    partial = weight_partial(inputs_t, prior_inputs_t[:, tokens - WINDOW :], own_grads, front_grads)
    owned = lax.psum_scatter(partial, ("seq", "lat"), scatter_dimension=0, tiled=True)
    q_width = HEADS * HEAD_DIM
    query_weight_grad = owned[:, :q_width]
    key_weight_grad = owned[:, q_width : q_width + kv_width]
    value_weight_grad = owned[:, q_width + kv_width :]
    return (input_grad, query_weight_grad, key_weight_grad, value_weight_grad)


def solution(mesh):
    placed = (
        P(("parts", "lat"), "seq", None),
        P(("parts", "lat"), "seq", None),
        P(("parts", "lat"), "seq", None),
        P(("parts", "lat"), "seq", None),
        P(("parts", "lat"), "seq", None),
        P(("parts", "lat"), "seq", None),
        P(),
        P(),
        P(),
    )
    return jax.shard_map(
        body,
        mesh=mesh,
        in_specs=placed,
        out_specs=(
            P(("parts", "lat"), "seq", None),
            P(("parts", "seq", "lat"), None),
            P(("parts", "seq", "lat"), None),
            P(("parts", "seq", "lat"), None),
        ),
        check_vma=False,
    )
```

```python
import jax
import jax.numpy as jnp
from jax import lax
from jax.experimental import pallas as pl
from jax.experimental.pallas import tpu as pltpu
from jax.sharding import PartitionSpec as P

HEADS = 16
HEAD_DIM = 64
KV_HEADS = 4
WINDOW = 512
ROW_BLOCK = 256


def shifted(block, axis, distance):
    devices = range(lax.axis_size(axis))
    route = [((i - distance) % len(devices), i) for i in devices]
    return lax.ppermute(block, axis, route)


def attn_kernel(q_ref, o_ref, do_ref, kp_ref, ko_ref, vp_ref, vo_ref, own_ref, front_ref,
                own32_ref, front32_ref, dk_scr, dv_scr, k_ref, v_ref):
    prior = kp_ref.shape[0]
    k_ref[:prior, :] = kp_ref[...]
    k_ref[prior:, :] = ko_ref[...]
    v_ref[:prior, :] = vp_ref[...]
    v_ref[prior:, :] = vo_ref[...]
    rows = q_ref.shape[0]
    ratio = HEADS // KV_HEADS
    scale = HEAD_DIM ** (-0.5)
    span = ROW_BLOCK + WINDOW
    q_width = HEADS * HEAD_DIM
    kv_width = KV_HEADS * HEAD_DIM
    stacked = ratio * ROW_BLOCK
    row = lax.broadcasted_iota(jnp.int32, (stacked, span), 0) % ROW_BLOCK
    col = lax.broadcasted_iota(jnp.int32, (stacked, span), 1)
    linked = (col > row) & (col <= row + WINDOW)
    by_rows = (((0,), (0,)), ((), ()))
    by_cols = (((1,), (1,)), ((), ()))
    for c in range(KV_HEADS):
        kv_cols = slice(c * HEAD_DIM, (c + 1) * HEAD_DIM)
        dk_scr[...] = jnp.zeros(dk_scr.shape, jnp.float32)
        dv_scr[...] = jnp.zeros(dv_scr.shape, jnp.float32)
        for a in range(rows // ROW_BLOCK):
            top = a * ROW_BLOCK
            keys = k_ref[top : top + span, kv_cols]
            values = v_ref[top : top + span, kv_cols]
            heads = [slice((c * ratio + r) * HEAD_DIM, (c * ratio + r + 1) * HEAD_DIM) for r in range(ratio)]
            q = jnp.concatenate([q_ref[top : top + ROW_BLOCK, sl] for sl in heads], axis=0)
            dout = jnp.concatenate([do_ref[top : top + ROW_BLOCK, sl] for sl in heads], axis=0)
            out = jnp.concatenate([o_ref[top : top + ROW_BLOCK, sl] for sl in heads], axis=0)
            q_scaled = q * jnp.asarray(scale, q.dtype)
            s = lax.dot_general(q_scaled, keys, by_cols, preferred_element_type=jnp.float32)
            s = jnp.where(linked, s, -jnp.inf)
            peak = jnp.max(s, axis=1, keepdims=True)
            raised = jnp.exp(s - peak)
            probs = raised * (1.0 / jnp.sum(raised, axis=1, keepdims=True))
            dp = lax.dot_general(dout, values, by_cols, preferred_element_type=jnp.float32)
            delta = jnp.sum(dout.astype(jnp.float32) * out.astype(jnp.float32), axis=1, keepdims=True)
            ds = (probs * (dp - delta)).astype(jnp.bfloat16)
            dq = jnp.dot(ds, keys, preferred_element_type=jnp.float32) * scale
            for r, sl in enumerate(heads):
                own_ref[top : top + ROW_BLOCK, sl] = dq[r * ROW_BLOCK : (r + 1) * ROW_BLOCK].astype(own_ref.dtype)
            dk_scr[:, top : top + span] += lax.dot_general(q, ds, by_rows, preferred_element_type=jnp.float32)
            dv_scr[:, top : top + span] += lax.dot_general(
                dout, probs.astype(jnp.bfloat16), by_rows, preferred_element_type=jnp.float32
            )
        dk_all = dk_scr[...].T * scale
        dv_all = dv_scr[...].T
        k_cols = slice(q_width + c * HEAD_DIM, q_width + (c + 1) * HEAD_DIM)
        v_cols = slice(q_width + kv_width + c * HEAD_DIM, q_width + kv_width + (c + 1) * HEAD_DIM)
        own_ref[:, k_cols] = dk_all[WINDOW:].astype(own_ref.dtype)
        own_ref[:, v_cols] = dv_all[WINDOW:].astype(own_ref.dtype)
        front_ref[:, kv_cols] = dk_all[:WINDOW].astype(front_ref.dtype)
        front_ref[:, slice(kv_width + c * HEAD_DIM, kv_width + (c + 1) * HEAD_DIM)] = (
            dv_all[:WINDOW].astype(front_ref.dtype)
        )
        own32_ref[0, :, kv_cols] = dk_all[WINDOW:]
        own32_ref[1, :, kv_cols] = dv_all[WINDOW:]
        front32_ref[0, :, kv_cols] = dk_all[:WINDOW]
        front32_ref[1, :, kv_cols] = dv_all[:WINDOW]


def attention_grads(queries, outputs, douts, prior_keys, keys_own, prior_values, values_own):
    rows, q_width = queries.shape
    prior, kv_width = prior_keys.shape
    span = prior + keys_own.shape[0]
    return pl.pallas_call(
        attn_kernel,
        out_shape=[
            jax.ShapeDtypeStruct((rows, q_width + 2 * kv_width), jnp.bfloat16),
            jax.ShapeDtypeStruct((prior, 2 * kv_width), jnp.bfloat16),
            jax.ShapeDtypeStruct((2, rows, kv_width), jnp.float32),
            jax.ShapeDtypeStruct((2, prior, kv_width), jnp.float32),
        ],
        scratch_shapes=[
            pltpu.VMEM((HEAD_DIM, span), jnp.float32),
            pltpu.VMEM((HEAD_DIM, span), jnp.float32),
            pltpu.VMEM((span, kv_width), prior_keys.dtype),
            pltpu.VMEM((span, kv_width), prior_values.dtype),
        ],
    )(queries, outputs, douts, prior_keys, keys_own, prior_values, values_own)


def wgrad_kernel(x_ref, xp_ref, own_ref, front_ref, out_ref):
    q_width = out_ref.shape[1] - front_ref.shape[1]
    own_part = jnp.dot(x_ref[...], own_ref[...], preferred_element_type=jnp.float32)
    front_part = jnp.dot(xp_ref[...], front_ref[...], preferred_element_type=jnp.float32)
    out_ref[:, :q_width] = own_part[:, :q_width]
    out_ref[:, q_width:] = own_part[:, q_width:] + front_part


def weight_partial(inputs_t, prior_inputs_t, own_grads, front_grads):
    model, tokens = inputs_t.shape
    width = own_grads.shape[1]
    cols = 256 if model % 256 == 0 else model
    x_block = pl.BlockSpec((cols, tokens), lambda i: (i, 0))
    return pl.pallas_call(
        wgrad_kernel,
        grid=(model // cols,),
        in_specs=[
            x_block,
            x_block,
            pl.BlockSpec(own_grads.shape, lambda i: (0, 0)),
            pl.BlockSpec(front_grads.shape, lambda i: (0, 0)),
        ],
        out_specs=pl.BlockSpec((cols, width), lambda i: (i, 0)),
        out_shape=jax.ShapeDtypeStruct((model, width), jnp.float32),
    )(inputs_t, prior_inputs_t, own_grads, front_grads)


def split_kernel(src_ref, q_out, k_out, v_out):
    q_width = q_out.shape[1]
    kv_width = k_out.shape[1]
    q_out[...] = src_ref[:, :q_width]
    k_out[...] = src_ref[:, q_width : q_width + kv_width]
    v_out[...] = src_ref[:, q_width + kv_width :]


def split_columns(owned, q_width, kv_width):
    rows = owned.shape[0]
    return pl.pallas_call(
        split_kernel,
        out_shape=[
            jax.ShapeDtypeStruct((rows, q_width), owned.dtype),
            jax.ShapeDtypeStruct((rows, kv_width), owned.dtype),
            jax.ShapeDtypeStruct((rows, kv_width), owned.dtype),
        ],
    )(owned)


def body(
    layer_input,
    query_rows,
    key_rows,
    value_rows,
    saved_output,
    output_grad,
    weight_query,
    weight_key,
    weight_value,
):
    inputs = layer_input[0]
    queries = query_rows[0]
    keys_own = key_rows[0]
    values_own = value_rows[0]
    outputs_own = saved_output[0]
    douts = output_grad[0]
    tokens = queries.shape[0]
    kv_width = keys_own.shape[1]
    prior_keys = shifted(keys_own, "seq", 1)
    prior_values = shifted(values_own, "seq", 1)
    inputs_t = inputs.T
    inputs_after, prior_keys, prior_values = lax.optimization_barrier(
        (inputs_t, prior_keys, prior_values)
    )
    prior_inputs_t = shifted(inputs_after, "seq", 1)
    own_grads, front_grads, own32, front32 = attention_grads(
        queries, outputs_own, douts, prior_keys, keys_own, prior_values, values_own
    )
    q_span = HEADS * HEAD_DIM
    query_blocks = own_grads[:, :q_span]
    returned = shifted(front32, "seq", -1)
    key_grad = own32[0].at[tokens - WINDOW :].add(returned[0]).astype(jnp.bfloat16)
    value_grad = own32[1].at[tokens - WINDOW :].add(returned[1]).astype(jnp.bfloat16)
    contract_cols = (((1,), (1,)), ((), ()))
    summed = lax.dot_general(
        query_blocks, weight_query, contract_cols, preferred_element_type=jnp.float32
    )
    summed = summed + lax.dot_general(
        key_grad, weight_key, contract_cols, preferred_element_type=jnp.float32
    )
    summed = summed + lax.dot_general(
        value_grad, weight_value, contract_cols, preferred_element_type=jnp.float32
    )
    input_grad = summed.astype(jnp.bfloat16)[None]
    partial = weight_partial(inputs_t, prior_inputs_t[:, tokens - WINDOW :], own_grads, front_grads)
    owned = lax.psum_scatter(partial, ("seq", "lat"), scatter_dimension=0, tiled=True)
    query_weight_grad, key_weight_grad, value_weight_grad = split_columns(
        owned, HEADS * HEAD_DIM, kv_width
    )
    return (input_grad, query_weight_grad, key_weight_grad, value_weight_grad)


def solution(mesh):
    placed = (
        P(("parts", "lat"), "seq", None),
        P(("parts", "lat"), "seq", None),
        P(("parts", "lat"), "seq", None),
        P(("parts", "lat"), "seq", None),
        P(("parts", "lat"), "seq", None),
        P(("parts", "lat"), "seq", None),
        P(),
        P(),
        P(),
    )
    return jax.shard_map(
        body,
        mesh=mesh,
        in_specs=placed,
        out_specs=(
            P(("parts", "lat"), "seq", None),
            P(("parts", "seq", "lat"), None),
            P(("parts", "seq", "lat"), None),
            P(("parts", "seq", "lat"), None),
        ),
        check_vma=False,
    )
```

```python
import jax
import jax.numpy as jnp
from jax import lax
from jax.experimental import pallas as pl
from jax.experimental.pallas import tpu as pltpu
from jax.sharding import PartitionSpec as P

HEADS = 16
HEAD_DIM = 64
KV_HEADS = 4
WINDOW = 512
ROW_BLOCK = 256


def shifted(block, axis, distance):
    devices = range(lax.axis_size(axis))
    route = [((i - distance) % len(devices), i) for i in devices]
    return lax.ppermute(block, axis, route)


def attn_kernel(q_ref, o_ref, do_ref, kp_ref, ko_ref, vp_ref, vo_ref, own_ref, front_ref,
                own32_ref, front32_ref, dk_scr, dv_scr, k_ref, v_ref):
    prior = kp_ref.shape[0]
    k_ref[:prior, :] = kp_ref[...]
    k_ref[prior:, :] = ko_ref[...]
    v_ref[:prior, :] = vp_ref[...]
    v_ref[prior:, :] = vo_ref[...]
    rows = q_ref.shape[0]
    ratio = HEADS // KV_HEADS
    scale = HEAD_DIM ** (-0.5)
    span = ROW_BLOCK + WINDOW
    q_width = HEADS * HEAD_DIM
    kv_width = KV_HEADS * HEAD_DIM
    stacked = ratio * ROW_BLOCK
    row = lax.broadcasted_iota(jnp.int32, (stacked, span), 0) % ROW_BLOCK
    col = lax.broadcasted_iota(jnp.int32, (stacked, span), 1)
    linked = (col > row) & (col <= row + WINDOW)
    by_rows = (((0,), (0,)), ((), ()))
    by_cols = (((1,), (1,)), ((), ()))
    for c in range(KV_HEADS):
        kv_cols = slice(c * HEAD_DIM, (c + 1) * HEAD_DIM)
        dk_scr[...] = jnp.zeros(dk_scr.shape, jnp.float32)
        dv_scr[...] = jnp.zeros(dv_scr.shape, jnp.float32)
        for a in range(rows // ROW_BLOCK):
            top = a * ROW_BLOCK
            keys = k_ref[top : top + span, kv_cols]
            values = v_ref[top : top + span, kv_cols]
            heads = [slice((c * ratio + r) * HEAD_DIM, (c * ratio + r + 1) * HEAD_DIM) for r in range(ratio)]
            q = jnp.concatenate([q_ref[top : top + ROW_BLOCK, sl] for sl in heads], axis=0)
            dout = jnp.concatenate([do_ref[top : top + ROW_BLOCK, sl] for sl in heads], axis=0)
            out = jnp.concatenate([o_ref[top : top + ROW_BLOCK, sl] for sl in heads], axis=0)
            q_scaled = q * jnp.asarray(scale, q.dtype)
            s = lax.dot_general(q_scaled, keys, by_cols, preferred_element_type=jnp.float32)
            s = jnp.where(linked, s, -jnp.inf)
            peak = jnp.max(s, axis=1, keepdims=True)
            raised = jnp.exp(s - peak)
            probs = raised * (1.0 / jnp.sum(raised, axis=1, keepdims=True))
            dp = lax.dot_general(dout, values, by_cols, preferred_element_type=jnp.float32)
            delta = jnp.sum(dout.astype(jnp.float32) * out.astype(jnp.float32), axis=1, keepdims=True)
            ds = (probs * (dp - delta)).astype(jnp.bfloat16)
            dq = jnp.dot(ds, keys, preferred_element_type=jnp.float32) * scale
            for r, sl in enumerate(heads):
                own_ref[top : top + ROW_BLOCK, sl] = dq[r * ROW_BLOCK : (r + 1) * ROW_BLOCK].astype(own_ref.dtype)
            dk_scr[:, top : top + span] += lax.dot_general(q, ds, by_rows, preferred_element_type=jnp.float32)
            dv_scr[:, top : top + span] += lax.dot_general(
                dout, probs.astype(jnp.bfloat16), by_rows, preferred_element_type=jnp.float32
            )
        dk_all = dk_scr[...].T * scale
        dv_all = dv_scr[...].T
        k_cols = slice(q_width + c * HEAD_DIM, q_width + (c + 1) * HEAD_DIM)
        v_cols = slice(q_width + kv_width + c * HEAD_DIM, q_width + kv_width + (c + 1) * HEAD_DIM)
        own_ref[:, k_cols] = dk_all[WINDOW:].astype(own_ref.dtype)
        own_ref[:, v_cols] = dv_all[WINDOW:].astype(own_ref.dtype)
        front_ref[:, kv_cols] = dk_all[:WINDOW].astype(front_ref.dtype)
        front_ref[:, slice(kv_width + c * HEAD_DIM, kv_width + (c + 1) * HEAD_DIM)] = (
            dv_all[:WINDOW].astype(front_ref.dtype)
        )
        own32_ref[0, :, kv_cols] = dk_all[WINDOW:]
        own32_ref[1, :, kv_cols] = dv_all[WINDOW:]
        front32_ref[0, :, kv_cols] = dk_all[:WINDOW]
        front32_ref[1, :, kv_cols] = dv_all[:WINDOW]


def attention_grads(queries, outputs, douts, prior_keys, keys_own, prior_values, values_own):
    rows, q_width = queries.shape
    prior, kv_width = prior_keys.shape
    span = prior + keys_own.shape[0]
    return pl.pallas_call(
        attn_kernel,
        out_shape=[
            jax.ShapeDtypeStruct((rows, q_width + 2 * kv_width), jnp.bfloat16),
            jax.ShapeDtypeStruct((prior, 2 * kv_width), jnp.bfloat16),
            jax.ShapeDtypeStruct((2, rows, kv_width), jnp.float32),
            jax.ShapeDtypeStruct((2, prior, kv_width), jnp.float32),
        ],
        scratch_shapes=[
            pltpu.VMEM((HEAD_DIM, span), jnp.float32),
            pltpu.VMEM((HEAD_DIM, span), jnp.float32),
            pltpu.VMEM((span, kv_width), prior_keys.dtype),
            pltpu.VMEM((span, kv_width), prior_values.dtype),
        ],
    )(queries, outputs, douts, prior_keys, keys_own, prior_values, values_own)


def wgrad_kernel(x_ref, xp_ref, own_ref, front_ref, out_ref):
    q_width = out_ref.shape[1] - front_ref.shape[1]
    own_part = jnp.dot(x_ref[...], own_ref[...], preferred_element_type=jnp.float32)
    front_part = jnp.dot(xp_ref[...], front_ref[...], preferred_element_type=jnp.float32)
    out_ref[:, :q_width] = own_part[:, :q_width]
    out_ref[:, q_width:] = own_part[:, q_width:] + front_part


def weight_partial(inputs_t, prior_inputs_t, own_grads, front_grads):
    model, tokens = inputs_t.shape
    width = own_grads.shape[1]
    cols = 512 if model % 512 == 0 else model
    x_block = pl.BlockSpec((cols, tokens), lambda i: (i, 0))
    return pl.pallas_call(
        wgrad_kernel,
        grid=(model // cols,),
        in_specs=[
            x_block,
            x_block,
            pl.BlockSpec(own_grads.shape, lambda i: (0, 0)),
            pl.BlockSpec(front_grads.shape, lambda i: (0, 0)),
        ],
        out_specs=pl.BlockSpec((cols, width), lambda i: (i, 0)),
        out_shape=jax.ShapeDtypeStruct((model, width), jnp.float32),
    )(inputs_t, prior_inputs_t, own_grads, front_grads)


def split_kernel(src_ref, q_out, k_out, v_out):
    q_width = q_out.shape[1]
    kv_width = k_out.shape[1]
    q_out[...] = src_ref[:, :q_width]
    k_out[...] = src_ref[:, q_width : q_width + kv_width]
    v_out[...] = src_ref[:, q_width + kv_width :]


def split_columns(owned, q_width, kv_width):
    rows = owned.shape[0]
    return pl.pallas_call(
        split_kernel,
        out_shape=[
            jax.ShapeDtypeStruct((rows, q_width), owned.dtype),
            jax.ShapeDtypeStruct((rows, kv_width), owned.dtype),
            jax.ShapeDtypeStruct((rows, kv_width), owned.dtype),
        ],
    )(owned)


def body(
    layer_input,
    query_rows,
    key_rows,
    value_rows,
    saved_output,
    output_grad,
    weight_query,
    weight_key,
    weight_value,
):
    inputs = layer_input[0]
    queries = query_rows[0]
    keys_own = key_rows[0]
    values_own = value_rows[0]
    outputs_own = saved_output[0]
    douts = output_grad[0]
    tokens = queries.shape[0]
    kv_width = keys_own.shape[1]
    prior_keys = shifted(keys_own, "seq", 1)
    prior_values = shifted(values_own, "seq", 1)
    inputs_t = inputs.T
    inputs_after, prior_keys, prior_values = lax.optimization_barrier(
        (inputs_t, prior_keys, prior_values)
    )
    prior_inputs_t = shifted(inputs_after, "seq", 1)
    own_grads, front_grads, own32, front32 = attention_grads(
        queries, outputs_own, douts, prior_keys, keys_own, prior_values, values_own
    )
    q_span = HEADS * HEAD_DIM
    query_blocks = own_grads[:, :q_span]
    returned = shifted(front32, "seq", -1)
    key_grad = own32[0].at[tokens - WINDOW :].add(returned[0]).astype(jnp.bfloat16)
    value_grad = own32[1].at[tokens - WINDOW :].add(returned[1]).astype(jnp.bfloat16)
    contract_cols = (((1,), (1,)), ((), ()))
    summed = lax.dot_general(
        query_blocks, weight_query, contract_cols, preferred_element_type=jnp.float32
    )
    summed = summed + lax.dot_general(
        key_grad, weight_key, contract_cols, preferred_element_type=jnp.float32
    )
    summed = summed + lax.dot_general(
        value_grad, weight_value, contract_cols, preferred_element_type=jnp.float32
    )
    input_grad = summed.astype(jnp.bfloat16)[None]
    partial = weight_partial(inputs_t, prior_inputs_t[:, tokens - WINDOW :], own_grads, front_grads)
    owned = lax.psum_scatter(partial, ("seq", "lat"), scatter_dimension=0, tiled=True)
    query_weight_grad, key_weight_grad, value_weight_grad = split_columns(
        owned, HEADS * HEAD_DIM, kv_width
    )
    return (input_grad, query_weight_grad, key_weight_grad, value_weight_grad)


def solution(mesh):
    placed = (
        P(("parts", "lat"), "seq", None),
        P(("parts", "lat"), "seq", None),
        P(("parts", "lat"), "seq", None),
        P(("parts", "lat"), "seq", None),
        P(("parts", "lat"), "seq", None),
        P(("parts", "lat"), "seq", None),
        P(),
        P(),
        P(),
    )
    return jax.shard_map(
        body,
        mesh=mesh,
        in_specs=placed,
        out_specs=(
            P(("parts", "lat"), "seq", None),
            P(("parts", "seq", "lat"), None),
            P(("parts", "seq", "lat"), None),
            P(("parts", "seq", "lat"), None),
        ),
        check_vma=False,
    )
```
